32 devices in a mesh: grp: 2 (over y), ub: 4 (over x, core), it: 4 (over z).
Axes of the slice: x: 2, y: 2, z: 4, core: 2. Of those that a mesh axis runs over, the one named last changes fastest.
Arguments:
- user_factors: float32 [2048, 128], P(('grp', 'ub')), parts along dimension 0, may hold values from -2.5 to 2.5
- item_factors: float32 [8192, 128], P(('grp', 'ub', 'it')), parts along dimension 0, may hold values from -2.5 to 2.5
- item_index: int32 [3, 2048, 32], P(None, ('grp', 'ub'), 'it'), parts along dimension 1, may hold values from 0 to 255
- labels: int32 [3, 2048, 32], P(None, ('grp', 'ub'), 'it'), parts along dimension 1, may hold values 0 or 1
- confidence: float32 [3, 2048, 32], P(None, ('grp', 'ub'), 'it'), parts along dimension 1, may hold values from 0.2 to 5
Outputs:
- users_out: float32 [2048, 128], P(('grp', 'ub')), parts along dimension 0
- items_out: float32 [8192, 128], P(('grp', 'ub', 'it')), parts along dimension 0
The draws below stay inside these ranges and needn't reach their ends.
There are 2 independent parts, one for each index of `grp`. The reference program is written for one: setup_inputs(seed, part) draws one part's arguments, and reference() takes and returns one part's arrays. A program takes and returns all parts, laid end to end along the dimension named above; each array names one. Nothing has to cross between parts.
Inputs may be any that keep to these rules, and one draw needn't show every extreme that they name: `item_index`: item indices count within a slab of 256 items.
All inputs are finite; a program needn't handle non-finite values. No bound on the sum of `labels` on one device may be relied on, other than what follows from the above.
Results may differ from the reference program's by a relative error of at most 0.00016.
Values sent between devices are 32-bit elements; how exact they have to be, the bound alone decides.
No kernel may reach another device: no remote copies, remote signals or barrier semaphores. Data moves between devices by JAX's collectives and lax.ppermute only.
A program may use at most 64 MiB of HBM per device.

```python
import math
import jax
import jax.numpy as jnp
from jax import lax

K = 128
USR_DEV = 256
IT_DEV = 256
NNZ = 8
STRATA = 3
INNER = 2
USERS = 1024
ITEMS = 4096
SLOTS = 32
N_UB = 4
N_IT = 4


def place_ends(drawn, own_key, low, largest):
    dims = drawn.shape
    index_at = [jax.random.randint(jax.random.fold_in(own_key, axis), (), 0, dims[axis]) for axis in range(len(dims))]
    drawn = drawn.at[tuple(index_at)].set(low)
    longest = dims.index(max(dims))
    index_at[longest] = (index_at[longest] + 1) % dims[longest]
    return drawn.at[tuple(index_at)].set(largest)


def block_scale(own_key, extent, split, low, largest):
    loudness, own = 1.0, jax.random.fold_in(own_key, 6)
    for dim, shards_of in split:
        heights = jnp.exp(jax.random.uniform(jax.random.fold_in(own, dim), (shards_of,), jnp.float32, low / len(split), largest / len(split)))
        loudness = loudness * jnp.repeat(heights, extent[dim] // shards_of).reshape([-1 if axis == dim else 1 for axis in range(len(extent))])
    return loudness


def normal_values(own_key, shape, deviation, reach, pieces=(), kind=jnp.bfloat16):
    factor_of = block_scale(own_key, shape, pieces, -0.22, 0.18) if pieces else 1.0
    array = jax.random.normal(own_key, shape, jnp.float32) * deviation * factor_of
    return jnp.minimum(jnp.maximum(array, -reach), reach).astype(kind)


def setup_inputs(seed: int = 0, part: int = 0) -> dict:
    splits = jax.random.split(jax.random.key(seed), 6)
    part_keys = jax.random.split(jax.random.fold_in(splits[5], part), 6)
    return {
        "user_factors": normal_values(part_keys[0], (USERS, K), 0.4, 2.5, ((0, 4),), jnp.float32),
        "item_factors": normal_values(part_keys[1], (ITEMS, K), 0.4, 2.5, ((0, 16),), jnp.float32),
        "item_index": place_ends(jax.random.randint(part_keys[2], (STRATA, USERS, SLOTS), 0, IT_DEV), jax.random.fold_in(part_keys[2], 1), 0, IT_DEV - 1).astype(jnp.int32),
        "labels": place_ends((jax.random.randint(part_keys[3], (STRATA, USERS, SLOTS), 0, 2) < 1).astype(jnp.int32), jax.random.fold_in(part_keys[3], 1), 0, 1),
        "confidence": jnp.clip(jnp.exp(math.log(5.0) - 3.218876 * jax.random.uniform(part_keys[4], (STRATA, USERS, SLOTS), jnp.float32) ** block_scale(part_keys[4], (STRATA, USERS, SLOTS), ((1, 4), (2, 4)), -0.2, 0.2)), 0.2, 5.0),
    }


LR_USER = 0.02
LR_ITEM = 0.05
LAMBDA_REG = 1.0


def residual_tile(user_rows, item_rows, weight, target):
    scores = jnp.dot(user_rows, item_rows.T, precision=lax.Precision.HIGHEST)
    return weight * jax.nn.sigmoid(scores) - target


def update_block(packed):
    user_rows, item_rows, columns, conf_rows, label_rows = packed
    row_ids = jnp.broadcast_to(jnp.arange(user_rows.shape[0], dtype=jnp.int32)[:, None], columns.shape)
    empty = jnp.zeros((user_rows.shape[0], item_rows.shape[0]), jnp.float32)
    weight = empty.at[row_ids, columns].add(conf_rows)
    target = empty.at[row_ids, columns].add(conf_rows * label_rows)
    for inner_step in range(INNER):
        residual = residual_tile(user_rows, item_rows, weight, target)
        gradient = jnp.dot(residual, item_rows, precision=lax.Precision.HIGHEST)
        user_rows = user_rows - LR_USER * (gradient + LAMBDA_REG * user_rows)
    residual = residual_tile(user_rows, item_rows, weight, target)
    item_grad = jnp.dot(residual.T, user_rows, precision=lax.Precision.HIGHEST)
    item_rows = item_rows - LR_ITEM * (item_grad + LAMBDA_REG * item_rows)
    return user_rows, item_rows


def reference(user_factors, item_factors, item_index, labels, confidence):
    block_items = N_IT * IT_DEV
    user_blocks = user_factors.reshape(N_UB, USR_DEV, K)
    blocks = item_factors.reshape(N_UB, block_items, K)
    offsets = (jnp.arange(SLOTS, dtype=jnp.int32) // NNZ) * IT_DEV
    for stratum in range(STRATA):
        columns = (item_index[stratum] + offsets[None, :]).astype(jnp.int32).reshape(N_UB, USR_DEV, SLOTS)
        conf_rows = confidence[stratum].reshape(N_UB, USR_DEV, SLOTS)
        label_rows = labels[stratum].astype(jnp.float32).reshape(N_UB, USR_DEV, SLOTS)
        paired = jnp.roll(blocks, stratum, axis=0)
        user_blocks, updated = lax.map(update_block, (user_blocks, paired, columns, conf_rows, label_rows))
        blocks = jnp.roll(updated, -stratum, axis=0)
    return user_blocks.reshape(USERS, K), blocks.reshape(ITEMS, K)
```

```python
import math

import jax
import jax.numpy as jnp
from jax import lax
from jax.sharding import PartitionSpec as P

INNER = 2


LR_USER = 0.02
LR_ITEM = 0.05
LAMBDA_REG = 1.0


def from_behind(block, axis, distance):
    devices = range(lax.axis_size(axis))
    route = [((i - distance) % len(devices), i) for i in devices]
    return lax.ppermute(block, axis, route)


def sum_over(block, axis):
    count = lax.axis_size(axis)
    step = 1
    while step < count:
        partner = lax.ppermute(block, axis, [(i, i ^ step) for i in range(count)])
        block = block + partner
        step *= 2
    return block


def residual_tile(user_rows, item_rows, weight, target):
    scores = jnp.dot(user_rows, item_rows.T, precision=lax.Precision.HIGHEST)
    return weight * jax.nn.sigmoid(scores) - target


def build_tiles(index_rows, label_rows, conf_rows, slab_width):
    user_count, slot_count = index_rows.shape
    block_rows = math.gcd(user_count, 128)
    nblocks = user_count // block_rows
    columns = jnp.arange(slab_width, dtype=jnp.int32)

    def one_block(packed):
        index_part, label_part, conf_part = packed
        matches = (index_part[:, :, None] == columns).astype(jnp.float32)
        paired = jnp.stack([conf_part, conf_part * label_part.astype(jnp.float32)], 0)
        return jnp.einsum("aun,unc->auc", paired, matches, precision=lax.Precision.HIGHEST)

    stacked = lax.map(
        one_block,
        (
            index_rows.reshape(nblocks, block_rows, slot_count),
            label_rows.reshape(nblocks, block_rows, slot_count),
            conf_rows.reshape(nblocks, block_rows, slot_count),
        ),
    )
    weight = stacked[:, 0].reshape(user_count, slab_width)
    target = stacked[:, 1].reshape(user_count, slab_width)
    return (weight, target)


def per_device(user_factors, item_factors, item_index, labels, confidence):
    strata = item_index.shape[0]
    user_rows = user_factors
    slab = item_factors
    for stratum in range(strata):
        if stratum > 0:
            slab = from_behind(slab, "ub", 1)
        weight, target = build_tiles(
            item_index[stratum], labels[stratum], confidence[stratum], slab.shape[0]
        )
        for inner_step in range(INNER):
            residual = residual_tile(user_rows, slab, weight, target)
            partial_grad = jnp.dot(residual, slab, precision=lax.Precision.HIGHEST)
            gradient = sum_over(partial_grad, "it")
            user_rows = user_rows - LR_USER * (gradient + LAMBDA_REG * user_rows)
        residual = residual_tile(user_rows, slab, weight, target)
        item_grad = lax.dot_general(
            residual, user_rows, (((0,), (0,)), ((), ())), precision=lax.Precision.HIGHEST
        )
        slab = slab - LR_ITEM * (item_grad + LAMBDA_REG * slab)
    slab = from_behind(slab, "ub", 1 - strata)
    return (user_rows, slab)


def solution(mesh):
    return jax.shard_map(
        per_device,
        mesh=mesh,
        in_specs=(
            P(("grp", "ub"), None),
            P(("grp", "ub", "it"), None),
            P(None, ("grp", "ub"), "it"),
            P(None, ("grp", "ub"), "it"),
            P(None, ("grp", "ub"), "it"),
        ),
        out_specs=(P(("grp", "ub"), None), P(("grp", "ub", "it"), None)),
        check_vma=False,
    )
```

```python
import jax
import jax.numpy as jnp
from jax import lax
from jax.sharding import PartitionSpec as P

INNER = 2


LR_USER = 0.02
LR_ITEM = 0.05
LAMBDA_REG = 1.0


def shifted(block, axis, distance):
    count = lax.axis_size(axis)
    route = [((i + distance) % count, i) for i in range(count)]
    return lax.ppermute(block, axis, route)


def residual_tile(user_rows, item_rows, weight, target):
    scores = jnp.dot(user_rows, item_rows.T, precision=lax.Precision.HIGHEST)
    return weight * jax.nn.sigmoid(scores) - target


def build_tiles(index_rows, signed_rows, slab_width):
    slabs, user_count, slot_count = index_rows.shape
    columns = jnp.arange(slab_width, dtype=jnp.float32)
    matches = index_rows[:, :, :, None] == columns
    weight = jnp.sum(jnp.where(matches, jnp.abs(signed_rows)[:, :, :, None], 0.0), axis=2)
    target = jnp.sum(jnp.where(matches, jnp.maximum(signed_rows, 0.0)[:, :, :, None], 0.0), axis=2)
    weight = jnp.transpose(weight, (1, 0, 2)).reshape(user_count, slabs * slab_width)
    target = jnp.transpose(target, (1, 0, 2)).reshape(user_count, slabs * slab_width)
    return weight, target


def per_device(user_factors, item_factors, item_index, labels, confidence):
    strata, user_count, slot_count = item_index.shape
    slab_rows, width = item_factors.shape
    signed = jnp.where(labels > 0, confidence, -confidence)
    packed = jnp.concatenate(
        [
            item_factors.reshape(-1),
            item_index.astype(jnp.float32).reshape(-1),
            signed.reshape(-1),
        ]
    )
    gathered = lax.all_gather(packed, "it")
    slabs = gathered.shape[0]
    cut = slab_rows * width
    slot_size = strata * user_count * slot_count
    block = gathered[:, :cut].reshape(slabs * slab_rows, width)
    index_all = gathered[:, cut : cut + slot_size].reshape(slabs, strata, user_count, slot_count)
    signed_all = gathered[:, cut + slot_size :].reshape(slabs, strata, user_count, slot_count)

    slot_data = []
    for stratum in range(strata):
        here = jnp.stack([index_all[:, stratum], signed_all[:, stratum]], 0)
        if stratum > 0:
            here = shifted(here, "ub", stratum)
        slot_data.append(here)

    user_rows = user_factors
    for stratum in range(strata):
        if stratum > 0:
            user_rows = shifted(user_rows, "ub", 1)
        weight, target = build_tiles(slot_data[stratum][0], slot_data[stratum][1], slab_rows)
        for inner_step in range(INNER):
            residual = residual_tile(user_rows, block, weight, target)
            gradient = jnp.dot(residual, block, precision=lax.Precision.HIGHEST)
            user_rows = user_rows - LR_USER * (gradient + LAMBDA_REG * user_rows)
        residual = residual_tile(user_rows, block, weight, target)
        item_grad = lax.dot_general(
            residual, user_rows, (((0,), (0,)), ((), ())), precision=lax.Precision.HIGHEST
        )
        block = block - LR_ITEM * (item_grad + LAMBDA_REG * block)
    user_rows = shifted(user_rows, "ub", 1 - strata)
    me = lax.axis_index("it")
    slab = lax.dynamic_slice_in_dim(block, me * slab_rows, slab_rows, 0)
    return (user_rows, slab)


def solution(mesh):
    return jax.shard_map(
        per_device,
        mesh=mesh,
        in_specs=(
            P(("grp", "ub"), None),
            P(("grp", "ub", "it"), None),
            P(None, ("grp", "ub"), "it"),
            P(None, ("grp", "ub"), "it"),
            P(None, ("grp", "ub"), "it"),
        ),
        out_specs=(P(("grp", "ub"), None), P(("grp", "ub", "it"), None)),
        check_vma=False,
    )
```

```python
import jax
import jax.numpy as jnp
from jax import lax
from jax.sharding import PartitionSpec as P

INNER = 2


LR_USER = 0.02
LR_ITEM = 0.05
LAMBDA_REG = 1.0


def shifted(block, axis, distance):
    count = lax.axis_size(axis)
    route = [((i + distance) % count, i) for i in range(count)]
    return lax.ppermute(block, axis, route)


def residual_tile(user_rows, item_rows, weight_t, target_t):
    scores_t = jnp.dot(item_rows, user_rows.T, precision=lax.Precision.HIGHEST)
    return weight_t * jax.nn.sigmoid(scores_t) - target_t


def build_tiles(index_rows, signed_rows, slab_width):
    slabs, slot_count, user_count = index_rows.shape
    columns = jnp.arange(slab_width, dtype=jnp.float32)[None, None, :, None]
    matches = index_rows[:, :, None, :] == columns
    weight = jnp.sum(jnp.where(matches, jnp.abs(signed_rows)[:, :, None, :], 0.0), axis=1)
    target = jnp.sum(jnp.where(matches, jnp.maximum(signed_rows, 0.0)[:, :, None, :], 0.0), axis=1)
    return weight.reshape(slabs * slab_width, user_count), target.reshape(slabs * slab_width, user_count)


def per_device(user_factors, item_factors, item_index, labels, confidence):
    strata, user_count, slot_count = item_index.shape
    slab_rows, width = item_factors.shape
    signed = jnp.where(labels > 0, confidence, -confidence)
    packed = jnp.concatenate(
        [
            item_factors.reshape(-1),
            jnp.transpose(item_index.astype(jnp.float32), (0, 2, 1)).reshape(-1),
            jnp.transpose(signed, (0, 2, 1)).reshape(-1),
        ]
    )
    gathered = lax.all_gather(packed, "it")
    slabs = gathered.shape[0]
    cut = slab_rows * width
    slot_size = strata * user_count * slot_count
    block = gathered[:, :cut].reshape(slabs * slab_rows, width)
    index_all = gathered[:, cut : cut + slot_size].reshape(slabs, strata, slot_count, user_count)
    signed_all = gathered[:, cut + slot_size :].reshape(slabs, strata, slot_count, user_count)

    slot_data = []
    for stratum in range(strata):
        here = jnp.stack([index_all[:, stratum], signed_all[:, stratum]], 0)
        if stratum > 0:
            here = shifted(here, "ub", stratum)
        slot_data.append(here)

    user_rows = user_factors
    for stratum in range(strata):
        if stratum > 0:
            user_rows = shifted(user_rows, "ub", 1)
        weight, target = build_tiles(slot_data[stratum][0], slot_data[stratum][1], slab_rows)
        for inner_step in range(INNER):
            residual_t = residual_tile(user_rows, block, weight, target)
            gradient = lax.dot_general(
                residual_t, block, (((0,), (0,)), ((), ())), precision=lax.Precision.HIGHEST
            )
            user_rows = user_rows - LR_USER * (gradient + LAMBDA_REG * user_rows)
        residual_t = residual_tile(user_rows, block, weight, target)
        item_grad = jnp.dot(residual_t, user_rows, precision=lax.Precision.HIGHEST)
        block = block - LR_ITEM * (item_grad + LAMBDA_REG * block)
    user_rows = shifted(user_rows, "ub", 1 - strata)
    me = lax.axis_index("it")
    slab = lax.dynamic_slice_in_dim(block, me * slab_rows, slab_rows, 0)
    return (user_rows, slab)


def solution(mesh):
    return jax.shard_map(
        per_device,
        mesh=mesh,
        in_specs=(
            P(("grp", "ub"), None),
            P(("grp", "ub", "it"), None),
            P(None, ("grp", "ub"), "it"),
            P(None, ("grp", "ub"), "it"),
            P(None, ("grp", "ub"), "it"),
        ),
        out_specs=(P(("grp", "ub"), None), P(("grp", "ub", "it"), None)),
        check_vma=False,
    )
```

```python
import jax
import jax.numpy as jnp
from jax import lax
from jax.sharding import PartitionSpec as P

INNER = 2
MATMUL_PRECISION = lax.Precision.HIGH


LR_USER = 0.02
LR_ITEM = 0.05
LAMBDA_REG = 1.0


def shifted(block, axis, distance):
    count = lax.axis_size(axis)
    route = [((i + distance) % count, i) for i in range(count)]
    return lax.ppermute(block, axis, route)


def residual_tile(user_rows, item_rows, weight_t, target_t):
    scores_t = jnp.dot(item_rows, user_rows.T, precision=MATMUL_PRECISION)
    return weight_t * jax.nn.sigmoid(scores_t) - target_t


def build_tiles(index_rows, signed_rows, slab_width):
    slabs, slot_count, user_count = index_rows.shape
    columns = jnp.arange(slab_width, dtype=jnp.float32)[None, None, :, None]
    matches = index_rows[:, :, None, :] == columns
    weight = jnp.sum(jnp.where(matches, jnp.abs(signed_rows)[:, :, None, :], 0.0), axis=1)
    target = jnp.sum(jnp.where(matches, jnp.maximum(signed_rows, 0.0)[:, :, None, :], 0.0), axis=1)
    return weight.reshape(slabs * slab_width, user_count), target.reshape(slabs * slab_width, user_count)


def per_device(user_factors, item_factors, item_index, labels, confidence):
    strata, user_count, slot_count = item_index.shape
    slab_rows, width = item_factors.shape
    signed = jnp.where(labels > 0, confidence, -confidence)
    packed = jnp.concatenate(
        [
            item_factors.reshape(-1),
            jnp.transpose(item_index.astype(jnp.float32), (0, 2, 1)).reshape(-1),
            jnp.transpose(signed, (0, 2, 1)).reshape(-1),
        ]
    )
    gathered = lax.all_gather(packed, "it")
    slabs = gathered.shape[0]
    cut = slab_rows * width
    slot_size = strata * user_count * slot_count
    block = gathered[:, :cut].reshape(slabs * slab_rows, width)
    index_all = gathered[:, cut : cut + slot_size].reshape(slabs, strata, slot_count, user_count)
    signed_all = gathered[:, cut + slot_size :].reshape(slabs, strata, slot_count, user_count)

    slot_data = []
    for stratum in range(strata):
        here = jnp.stack([index_all[:, stratum], signed_all[:, stratum]], 0)
        if stratum > 0:
            here = shifted(here, "ub", stratum)
        slot_data.append(here)

    user_rows = user_factors
    for stratum in range(strata):
        if stratum > 0:
            user_rows = shifted(user_rows, "ub", 1)
        weight, target = build_tiles(slot_data[stratum][0], slot_data[stratum][1], slab_rows)
        for inner_step in range(INNER):
            residual_t = residual_tile(user_rows, block, weight, target)
            gradient = lax.dot_general(
                residual_t, block, (((0,), (0,)), ((), ())), precision=MATMUL_PRECISION
            )
            user_rows = user_rows - LR_USER * (gradient + LAMBDA_REG * user_rows)
        residual_t = residual_tile(user_rows, block, weight, target)
        item_grad = jnp.dot(residual_t, user_rows, precision=MATMUL_PRECISION)
        block = block - LR_ITEM * (item_grad + LAMBDA_REG * block)
    user_rows = shifted(user_rows, "ub", 1 - strata)
    me = lax.axis_index("it")
    slab = lax.dynamic_slice_in_dim(block, me * slab_rows, slab_rows, 0)
    return (user_rows, slab)


def solution(mesh):
    return jax.shard_map(
        per_device,
        mesh=mesh,
        in_specs=(
            P(("grp", "ub"), None),
            P(("grp", "ub", "it"), None),
            P(None, ("grp", "ub"), "it"),
            P(None, ("grp", "ub"), "it"),
            P(None, ("grp", "ub"), "it"),
        ),
        out_specs=(P(("grp", "ub"), None), P(("grp", "ub", "it"), None)),
        check_vma=False,
    )
```

```python
import jax
import jax.numpy as jnp
from jax import lax
from jax.sharding import PartitionSpec as P

INNER = 2
MATMUL_PRECISION = lax.Precision.HIGH


LR_USER = 0.02
LR_ITEM = 0.05
LAMBDA_REG = 1.0


def shifted(block, axis, distance):
    count = lax.axis_size(axis)
    route = [((i + distance) % count, i) for i in range(count)]
    return lax.ppermute(block, axis, route)


def gather_over(block, axis):
    count = lax.axis_size(axis)
    me = lax.axis_index(axis)
    received = [block] + [
        lax.ppermute(block, axis, [(i, i ^ k) for i in range(count)]) for k in range(1, count)
    ]
    order = jnp.arange(count, dtype=jnp.int32) ^ me
    return jnp.take(jnp.stack(received), order, axis=0)


def residual_tile(user_rows, item_rows, weight_t, target_t):
    scores_t = jnp.dot(item_rows, user_rows.T, precision=MATMUL_PRECISION)
    return weight_t * jax.nn.sigmoid(scores_t) - target_t


def build_tiles(index_rows, signed_rows, slab_width):
    slabs, slot_count, user_count = index_rows.shape
    columns = jnp.arange(slab_width, dtype=jnp.float32)[None, None, :, None]
    matches = index_rows[:, :, None, :] == columns
    weight = jnp.sum(jnp.where(matches, jnp.abs(signed_rows)[:, :, None, :], 0.0), axis=1)
    target = jnp.sum(jnp.where(matches, jnp.maximum(signed_rows, 0.0)[:, :, None, :], 0.0), axis=1)
    return weight.reshape(slabs * slab_width, user_count), target.reshape(slabs * slab_width, user_count)


def per_device(user_factors, item_factors, item_index, labels, confidence):
    strata, user_count, slot_count = item_index.shape
    slab_rows, width = item_factors.shape
    signed = jnp.where(labels > 0, confidence, -confidence)
    slots_local = jnp.stack(
        [jnp.transpose(item_index.astype(jnp.float32), (0, 2, 1)), jnp.transpose(signed, (0, 2, 1))], 1
    )
    slots_all = gather_over(slots_local, "it")
    slabs = slots_all.shape[0]
    block = gather_over(item_factors, "it").reshape(slabs * slab_rows, width)
    index_all = slots_all[:, :, 0]
    signed_all = slots_all[:, :, 1]

    slot_data = []
    for stratum in range(strata):
        here = jnp.stack([index_all[:, stratum], signed_all[:, stratum]], 0)
        if stratum > 0:
            here = shifted(here, "ub", stratum)
        slot_data.append(here)

    user_rows = user_factors
    for stratum in range(strata):
        if stratum > 0:
            user_rows = shifted(user_rows, "ub", 1)
        weight, target = build_tiles(slot_data[stratum][0], slot_data[stratum][1], slab_rows)
        for inner_step in range(INNER):
            residual_t = residual_tile(user_rows, block, weight, target)
            gradient = lax.dot_general(
                residual_t, block, (((0,), (0,)), ((), ())), precision=MATMUL_PRECISION
            )
            user_rows = user_rows - LR_USER * (gradient + LAMBDA_REG * user_rows)
        residual_t = residual_tile(user_rows, block, weight, target)
        item_grad = jnp.dot(residual_t, user_rows, precision=MATMUL_PRECISION)
        block = block - LR_ITEM * (item_grad + LAMBDA_REG * block)
    user_rows = shifted(user_rows, "ub", 1 - strata)
    me = lax.axis_index("it")
    slab = lax.dynamic_slice_in_dim(block, me * slab_rows, slab_rows, 0)
    return (user_rows, slab)


def solution(mesh):
    return jax.shard_map(
        per_device,
        mesh=mesh,
        in_specs=(
            P(("grp", "ub"), None),
            P(("grp", "ub", "it"), None),
            P(None, ("grp", "ub"), "it"),
            P(None, ("grp", "ub"), "it"),
            P(None, ("grp", "ub"), "it"),
        ),
        out_specs=(P(("grp", "ub"), None), P(("grp", "ub", "it"), None)),
        check_vma=False,
    )
```

```python
import jax
import jax.numpy as jnp
from jax import lax
from jax.sharding import PartitionSpec as P

INNER = 2
MATMUL_PRECISION = lax.Precision.HIGH


LR_USER = 0.02
LR_ITEM = 0.05
LAMBDA_REG = 1.0


def shifted(block, axis, distance):
    count = lax.axis_size(axis)
    route = [((i + distance) % count, i) for i in range(count)]
    return lax.ppermute(block, axis, route)


def gather_over(block, axis):
    count = lax.axis_size(axis)
    me = lax.axis_index(axis)
    received = [block] + [
        lax.ppermute(block, axis, [(i, i ^ k) for i in range(count)]) for k in range(1, count)
    ]
    order = jnp.arange(count, dtype=jnp.int32) ^ me
    return jnp.take(jnp.stack(received), order, axis=0)


def residual_tile(user_rows, item_rows, weight_t, target_t):
    scores_t = jnp.dot(item_rows, user_rows.T, precision=MATMUL_PRECISION)
    return weight_t * jax.nn.sigmoid(scores_t) - target_t


def build_tiles(index_rows, signed_rows, slab_width):
    slabs, slot_count, user_count = index_rows.shape
    columns = jnp.arange(slab_width, dtype=jnp.float32)[None, None, :, None]
    matches = index_rows[:, :, None, :] == columns
    weight = jnp.sum(jnp.where(matches, jnp.abs(signed_rows)[:, :, None, :], 0.0), axis=1)
    target = jnp.sum(jnp.where(matches, jnp.maximum(signed_rows, 0.0)[:, :, None, :], 0.0), axis=1)
    return weight.reshape(slabs * slab_width, user_count), target.reshape(slabs * slab_width, user_count)


def per_device(user_factors, item_factors, item_index, labels, confidence):
    strata, user_count, slot_count = item_index.shape
    slab_rows, width = item_factors.shape
    signed = jnp.where(labels > 0, confidence, -confidence)
    slots_local = jnp.stack(
        [jnp.transpose(item_index.astype(jnp.float32), (0, 2, 1)), jnp.transpose(signed, (0, 2, 1))], 1
    )
    slots_all = gather_over(slots_local, "it")
    slabs = slots_all.shape[0]
    block = gather_over(item_factors, "it").reshape(slabs * slab_rows, width)
    index_all = slots_all[:, :, 0]
    signed_all = slots_all[:, :, 1]

    slot_data = []
    for stratum in range(strata):
        here = jnp.stack([index_all[:, stratum], signed_all[:, stratum]], 0)
        if stratum > 0:
            here = shifted(here, "ub", stratum)
        slot_data.append(here)

    pieces = 2 if user_count % 256 == 0 else 1
    rows = user_count // pieces
    chunks = [user_factors[k * rows : (k + 1) * rows] for k in range(pieces)]
    for stratum in range(strata):
        if stratum > 0:
            chunks = [shifted(chunk, "ub", 1) for chunk in chunks]
        weight, target = build_tiles(slot_data[stratum][0], slot_data[stratum][1], slab_rows)
        finished = []
        residuals = []
        for k, chunk in enumerate(chunks):
            weight_k = weight[:, k * rows : (k + 1) * rows]
            target_k = target[:, k * rows : (k + 1) * rows]
            for inner_step in range(INNER):
                residual_t = residual_tile(chunk, block, weight_k, target_k)
                gradient = lax.dot_general(
                    residual_t, block, (((0,), (0,)), ((), ())), precision=MATMUL_PRECISION
                )
                chunk = chunk - LR_USER * (gradient + LAMBDA_REG * chunk)
            finished.append(chunk)
            residuals.append(residual_tile(chunk, block, weight_k, target_k))
        chunks = finished
        residual_t = jnp.concatenate(residuals, 1)
        item_grad = jnp.dot(residual_t, jnp.concatenate(chunks, 0), precision=MATMUL_PRECISION)
        block = block - LR_ITEM * (item_grad + LAMBDA_REG * block)
    user_rows = jnp.concatenate([shifted(chunk, "ub", 1 - strata) for chunk in chunks], 0)
    me = lax.axis_index("it")
    slab = lax.dynamic_slice_in_dim(block, me * slab_rows, slab_rows, 0)
    return (user_rows, slab)


def solution(mesh):
    return jax.shard_map(
        per_device,
        mesh=mesh,
        in_specs=(
            P(("grp", "ub"), None),
            P(("grp", "ub", "it"), None),
            P(None, ("grp", "ub"), "it"),
            P(None, ("grp", "ub"), "it"),
            P(None, ("grp", "ub"), "it"),
        ),
        out_specs=(P(("grp", "ub"), None), P(("grp", "ub", "it"), None)),
        check_vma=False,
    )
```

```python
import jax
import jax.numpy as jnp
from jax import lax
from jax.experimental import pallas as pl
from jax.experimental.pallas import tpu as pltpu
from jax.sharding import PartitionSpec as P

INNER = 2
MATMUL_PRECISION = lax.Precision.HIGH


LR_USER = 0.02
LR_ITEM = 0.05
LAMBDA_REG = 1.0


def shifted(block, axis, distance):
    count = lax.axis_size(axis)
    route = [((i + distance) % count, i) for i in range(count)]
    return lax.ppermute(block, axis, route)


def gather_over(block, axis):
    count = lax.axis_size(axis)
    me = lax.axis_index(axis)
    received = [block] + [
        lax.ppermute(block, axis, [(i, i ^ k) for i in range(count)]) for k in range(1, count)
    ]
    order = jnp.arange(count, dtype=jnp.int32) ^ me
    return jnp.take(jnp.stack(received), order, axis=0)


def residual_tile(user_rows, item_rows, weight_t, target_t):
    scores_t = jnp.dot(item_rows, user_rows.T, precision=MATMUL_PRECISION)
    return weight_t * jax.nn.sigmoid(scores_t) - target_t


def build_tiles(index_rows, signed_rows, slab_width, pieces):
    slabs, slot_count, user_count = index_rows.shape
    rows = user_count // pieces
    index_rows = jnp.transpose(index_rows.reshape(slabs, slot_count, pieces, rows), (2, 0, 1, 3))
    signed_rows = jnp.transpose(signed_rows.reshape(slabs, slot_count, pieces, rows), (2, 0, 1, 3))
    columns = jnp.arange(slab_width, dtype=jnp.float32)[None, None, None, :, None]
    matches = index_rows[:, :, :, None, :] == columns
    weight = jnp.sum(jnp.where(matches, jnp.abs(signed_rows)[:, :, :, None, :], 0.0), axis=2)
    target = jnp.sum(jnp.where(matches, jnp.maximum(signed_rows, 0.0)[:, :, :, None, :], 0.0), axis=2)
    return weight.reshape(pieces, slabs * slab_width, rows), target.reshape(pieces, slabs * slab_width, rows)


def user_steps_kernel(p_ref, q_ref, w_ref, t_ref, p_out, r_out):
    q = q_ref[...]
    w = w_ref[...]
    t = t_ref[...]

    def residual(p):
        scores_t = lax.dot_general(
            q, p, (((1,), (1,)), ((), ())), precision=lax.Precision.HIGHEST, preferred_element_type=jnp.float32
        )
        return w * jax.nn.sigmoid(scores_t) - t

    p = p_ref[...]
    for inner_step in range(INNER):
        gradient = lax.dot_general(
            residual(p), q, (((0,), (0,)), ((), ())), precision=lax.Precision.HIGHEST,
            preferred_element_type=jnp.float32,
        )
        p = p - LR_USER * (gradient + LAMBDA_REG * p)
    p_out[...] = p
    r_out[...] = residual(p)


def user_steps(chunk, block, weight, target):
    rows, width = chunk.shape
    items = block.shape[0]
    vmem = pl.BlockSpec(memory_space=pltpu.VMEM)
    flops = (2 * INNER + 1) * 2 * items * rows * width
    return pl.pallas_call(
        user_steps_kernel,
        out_shape=(
            jax.ShapeDtypeStruct((rows, width), jnp.float32),
            jax.ShapeDtypeStruct((items, rows), jnp.float32),
        ),
        in_specs=[vmem, vmem, vmem, vmem],
        out_specs=(vmem, vmem),
        cost_estimate=pl.CostEstimate(
            flops=6 * flops,
            transcendentals=(INNER + 1) * items * rows,
            bytes_accessed=4 * (2 * rows * width + items * width + 3 * items * rows),
        ),
    )(chunk, block, weight, target)


def per_device(user_factors, item_factors, item_index, labels, confidence):
    strata, user_count, slot_count = item_index.shape
    slab_rows, width = item_factors.shape
    signed = jnp.where(labels > 0, confidence, -confidence)
    slots_local = jnp.stack(
        [jnp.transpose(item_index.astype(jnp.float32), (0, 2, 1)), jnp.transpose(signed, (0, 2, 1))], 1
    )
    slots_all = gather_over(slots_local, "it")
    slabs = slots_all.shape[0]
    block = gather_over(item_factors, "it").reshape(slabs * slab_rows, width)
    index_all = slots_all[:, :, 0]
    signed_all = slots_all[:, :, 1]

    slot_data = []
    for stratum in range(strata):
        here = jnp.stack([index_all[:, stratum], signed_all[:, stratum]], 0)
        if stratum > 0:
            here = shifted(here, "ub", stratum)
        slot_data.append(here)

    pieces = 2 if user_count % 256 == 0 else 1
    rows = user_count // pieces
    chunks = [user_factors[k * rows : (k + 1) * rows] for k in range(pieces)]
    for stratum in range(strata):
        if stratum > 0:
            chunks = [shifted(chunk, "ub", 1) for chunk in chunks]
        weight, target = build_tiles(slot_data[stratum][0], slot_data[stratum][1], slab_rows, pieces)
        finished = []
        residuals = []
        for k, chunk in enumerate(chunks):
            chunk, residual_k = user_steps(chunk, block, weight[k], target[k])
            finished.append(chunk)
            residuals.append(residual_k)
        chunks = finished
        residual_t = jnp.concatenate(residuals, 1)
        item_grad = jnp.dot(residual_t, jnp.concatenate(chunks, 0), precision=MATMUL_PRECISION)
        block = block - LR_ITEM * (item_grad + LAMBDA_REG * block)
    user_rows = jnp.concatenate([shifted(chunk, "ub", 1 - strata) for chunk in chunks], 0)
    me = lax.axis_index("it")
    slab = lax.dynamic_slice_in_dim(block, me * slab_rows, slab_rows, 0)
    return (user_rows, slab)


def solution(mesh):
    return jax.shard_map(
        per_device,
        mesh=mesh,
        in_specs=(
            P(("grp", "ub"), None),
            P(("grp", "ub", "it"), None),
            P(None, ("grp", "ub"), "it"),
            P(None, ("grp", "ub"), "it"),
            P(None, ("grp", "ub"), "it"),
        ),
        out_specs=(P(("grp", "ub"), None), P(("grp", "ub", "it"), None)),
        check_vma=False,
    )
```

```python
import jax
import jax.numpy as jnp
from jax import lax
from jax.experimental import pallas as pl
from jax.experimental.pallas import tpu as pltpu
from jax.sharding import PartitionSpec as P

INNER = 2
MATMUL_PRECISION = lax.Precision.HIGH


LR_USER = 0.02
LR_ITEM = 0.05
LAMBDA_REG = 1.0


def shifted(block, axis, distance):
    count = lax.axis_size(axis)
    route = [((i + distance) % count, i) for i in range(count)]
    return lax.ppermute(block, axis, route)


def gather_over(block, axis):
    count = lax.axis_size(axis)
    me = lax.axis_index(axis)
    received = [block] + [
        lax.ppermute(block, axis, [(i, i ^ k) for i in range(count)]) for k in range(1, count)
    ]
    order = jnp.arange(count, dtype=jnp.int32) ^ me
    return jnp.take(jnp.stack(received), order, axis=0)


def residual_tile(user_rows, item_rows, weight_t, target_t):
    scores_t = jnp.dot(item_rows, user_rows.T, precision=MATMUL_PRECISION)
    return weight_t * jax.nn.sigmoid(scores_t) - target_t


def build_tiles(index_rows, signed_rows, slab_width):
    slabs, slot_count, user_count = index_rows.shape
    columns = jnp.arange(slab_width, dtype=jnp.float32)[None, None, :, None]
    matches = index_rows[:, :, None, :] == columns
    weight = jnp.sum(jnp.where(matches, jnp.abs(signed_rows)[:, :, None, :], 0.0), axis=1)
    target = jnp.sum(jnp.where(matches, jnp.maximum(signed_rows, 0.0)[:, :, None, :], 0.0), axis=1)
    return weight.reshape(slabs * slab_width, user_count), target.reshape(slabs * slab_width, user_count)


def split_bf16(x):
    high = x.astype(jnp.bfloat16)
    return high, (x - high.astype(jnp.float32)).astype(jnp.bfloat16)


def dot_three(a_parts, b_parts, dims):
    def one(a, b):
        return lax.dot_general(a, b, dims, preferred_element_type=jnp.float32)

    return one(a_parts[0], b_parts[0]) + (one(a_parts[0], b_parts[1]) + one(a_parts[1], b_parts[0]))


def user_steps_kernel(p_ref, q_ref, w_ref, t_ref, p_out, r_out):
    q = q_ref[...]
    q_parts = split_bf16(q)
    w = w_ref[...]
    t = t_ref[...]
    rows_by_rows = (((1,), (1,)), ((), ()))
    plain = (((1,), (0,)), ((), ()))

    def residual(p):
        scores_t = dot_three(q_parts, split_bf16(p), rows_by_rows)
        return w * jax.nn.sigmoid(scores_t) - t

    p = p_ref[...]
    for inner_step in range(INNER):
        residual_rows = residual(p).T
        gradient = dot_three(split_bf16(residual_rows), q_parts, plain)
        p = p - LR_USER * (gradient + LAMBDA_REG * p)
    p_out[...] = p
    r_out[...] = residual(p)


def user_steps(chunk, block, weight, target, piece):
    rows, width = chunk.shape
    items = block.shape[0]
    vmem = pl.BlockSpec(memory_space=pltpu.VMEM)
    columns = pl.BlockSpec((items, rows), lambda step: (0, piece))
    flops = (2 * INNER + 1) * 2 * items * rows * width
    return pl.pallas_call(
        user_steps_kernel,
        grid=(1,),
        out_shape=(
            jax.ShapeDtypeStruct((rows, width), jnp.float32),
            jax.ShapeDtypeStruct((items, rows), jnp.float32),
        ),
        in_specs=[vmem, vmem, columns, columns],
        out_specs=(vmem, vmem),
        cost_estimate=pl.CostEstimate(
            flops=3 * flops,
            transcendentals=(INNER + 1) * items * rows,
            bytes_accessed=4 * (2 * rows * width + items * width + 3 * items * rows),
        ),
    )(chunk, block, weight, target)


def per_device(user_factors, item_factors, item_index, labels, confidence):
    strata, user_count, slot_count = item_index.shape
    slab_rows, width = item_factors.shape
    signed = jnp.where(labels > 0, confidence, -confidence)
    slots_local = jnp.stack(
        [jnp.transpose(item_index.astype(jnp.float32), (0, 2, 1)), jnp.transpose(signed, (0, 2, 1))], 1
    )
    slots_all = gather_over(slots_local, "it")
    slabs = slots_all.shape[0]
    block = gather_over(item_factors, "it").reshape(slabs * slab_rows, width)
    index_all = slots_all[:, :, 0]
    signed_all = slots_all[:, :, 1]

    slot_data = []
    for stratum in range(strata):
        here = jnp.stack([index_all[:, stratum], signed_all[:, stratum]], 0)
        if stratum > 0:
            here = shifted(here, "ub", stratum)
        slot_data.append(here)

    pieces = 2 if user_count % 256 == 0 else 1
    rows = user_count // pieces
    chunks = [user_factors[k * rows : (k + 1) * rows] for k in range(pieces)]
    for stratum in range(strata):
        if stratum > 0:
            chunks = [shifted(chunk, "ub", 1) for chunk in chunks]
        weight, target = build_tiles(slot_data[stratum][0], slot_data[stratum][1], slab_rows)
        finished = []
        residuals = []
        for k, chunk in enumerate(chunks):
            chunk, residual_k = user_steps(chunk, block, weight, target, k)
            finished.append(chunk)
            residuals.append(residual_k)
        chunks = finished
        residual_t = jnp.concatenate(residuals, 1)
        item_grad = jnp.dot(residual_t, jnp.concatenate(chunks, 0), precision=MATMUL_PRECISION)
        block = block - LR_ITEM * (item_grad + LAMBDA_REG * block)
    user_rows = jnp.concatenate([shifted(chunk, "ub", 1 - strata) for chunk in chunks], 0)
    me = lax.axis_index("it")
    slab = lax.dynamic_slice_in_dim(block, me * slab_rows, slab_rows, 0)
    return (user_rows, slab)


def solution(mesh):
    return jax.shard_map(
        per_device,
        mesh=mesh,
        in_specs=(
            P(("grp", "ub"), None),
            P(("grp", "ub", "it"), None),
            P(None, ("grp", "ub"), "it"),
            P(None, ("grp", "ub"), "it"),
            P(None, ("grp", "ub"), "it"),
        ),
        out_specs=(P(("grp", "ub"), None), P(("grp", "ub", "it"), None)),
        check_vma=False,
    )
```

```python
import jax
import jax.numpy as jnp
from jax import lax
from jax.sharding import PartitionSpec as P

INNER = 2
MATMUL_PRECISION = lax.Precision.HIGH


LR_USER = 0.02
LR_ITEM = 0.05
LAMBDA_REG = 1.0


def shifted(block, axis, distance):
    count = lax.axis_size(axis)
    route = [((i + distance) % count, i) for i in range(count)]
    return lax.ppermute(block, axis, route)


def gather_over(block, axis):
    count = lax.axis_size(axis)
    me = lax.axis_index(axis)
    received = [block] + [
        lax.ppermute(block, axis, [(i, i ^ k) for i in range(count)]) for k in range(1, count)
    ]
    order = jnp.arange(count, dtype=jnp.int32) ^ me
    return jnp.take(jnp.stack(received), order, axis=0)


def residual_tile(user_rows, item_rows, weight_t, target_t):
    scores_t = jnp.dot(item_rows, user_rows.T, precision=MATMUL_PRECISION)
    return weight_t * jax.nn.sigmoid(scores_t) - target_t


def build_tiles(index_rows, signed_rows, slab_width):
    slabs, slot_count, user_count = index_rows.shape
    columns = jnp.arange(slab_width, dtype=jnp.float32)[None, None, :, None]
    matches = index_rows[:, :, None, :] == columns
    weight = jnp.sum(jnp.where(matches, jnp.abs(signed_rows)[:, :, None, :], 0.0), axis=1)
    target = jnp.sum(jnp.where(matches, jnp.maximum(signed_rows, 0.0)[:, :, None, :], 0.0), axis=1)
    return weight.reshape(slabs * slab_width, user_count), target.reshape(slabs * slab_width, user_count)


def per_device(user_factors, item_factors, item_index, labels, confidence):
    strata, user_count, slot_count = item_index.shape
    slab_rows, width = item_factors.shape
    signed = jnp.where(labels > 0, confidence, -confidence)
    slots_local = jnp.stack(
        [jnp.transpose(item_index.astype(jnp.float32), (0, 2, 1)), jnp.transpose(signed, (0, 2, 1))], 1
    )
    slots_all = gather_over(slots_local, "it")
    slabs = slots_all.shape[0]
    block = gather_over(item_factors, "it").reshape(slabs * slab_rows, width)
    index_all = slots_all[:, :, 0]
    signed_all = slots_all[:, :, 1]

    slot_data = []
    for stratum in range(strata):
        here = jnp.stack([index_all[:, stratum], signed_all[:, stratum]], 0)
        if stratum > 0:
            here = shifted(here, "ub", stratum)
        slot_data.append(here)

    pieces = 2 if user_count % 256 == 0 else 1
    rows = user_count // pieces
    chunks = [user_factors[k * rows : (k + 1) * rows] for k in range(pieces)]
    for stratum in range(strata):
        if stratum > 0:
            chunks = [shifted(chunk, "ub", 1) for chunk in chunks]
        weight, target = build_tiles(slot_data[stratum][0], slot_data[stratum][1], slab_rows)
        finished = []
        residuals = []
        for k, chunk in enumerate(chunks):
            weight_k = weight[:, k * rows : (k + 1) * rows]
            target_k = target[:, k * rows : (k + 1) * rows]
            for inner_step in range(INNER):
                residual_t = residual_tile(chunk, block, weight_k, target_k)
                gradient = lax.dot_general(
                    residual_t, block, (((0,), (0,)), ((), ())), precision=MATMUL_PRECISION
                )
                chunk = chunk - LR_USER * (gradient + LAMBDA_REG * chunk)
            if k == 0 and stratum + 1 < strata:
                slot_data[stratum + 1], chunk = lax.optimization_barrier((slot_data[stratum + 1], chunk))
            finished.append(chunk)
            residuals.append(residual_tile(chunk, block, weight_k, target_k))
        chunks = finished
        residual_t = jnp.concatenate(residuals, 1)
        item_grad = jnp.dot(residual_t, jnp.concatenate(chunks, 0), precision=MATMUL_PRECISION)
        block = block - LR_ITEM * (item_grad + LAMBDA_REG * block)
    user_rows = jnp.concatenate([shifted(chunk, "ub", 1 - strata) for chunk in chunks], 0)
    me = lax.axis_index("it")
    slab = lax.dynamic_slice_in_dim(block, me * slab_rows, slab_rows, 0)
    return (user_rows, slab)


def solution(mesh):
    return jax.shard_map(
        per_device,
        mesh=mesh,
        in_specs=(
            P(("grp", "ub"), None),
            P(("grp", "ub", "it"), None),
            P(None, ("grp", "ub"), "it"),
            P(None, ("grp", "ub"), "it"),
            P(None, ("grp", "ub"), "it"),
        ),
        out_specs=(P(("grp", "ub"), None), P(("grp", "ub", "it"), None)),
        check_vma=False,
    )
```

```python
import jax
import jax.numpy as jnp
from jax import lax
from jax.sharding import PartitionSpec as P

INNER = 2
MATMUL_PRECISION = lax.Precision.HIGH


LR_USER = 0.02
LR_ITEM = 0.05
LAMBDA_REG = 1.0


def shifted(block, axis, distance):
    count = lax.axis_size(axis)
    route = [((i + distance) % count, i) for i in range(count)]
    return lax.ppermute(block, axis, route)


def gather_over(block, axis):
    count = lax.axis_size(axis)
    me = lax.axis_index(axis)
    received = [block] + [
        lax.ppermute(block, axis, [(i, i ^ k) for i in range(count)]) for k in range(1, count)
    ]
    order = jnp.arange(count, dtype=jnp.int32) ^ me
    return jnp.take(jnp.stack(received), order, axis=0)


def residual_tile(user_rows, item_rows, weight_t, target_t):
    scores_t = jnp.dot(item_rows, user_rows.T, precision=MATMUL_PRECISION)
    return weight_t * jax.nn.sigmoid(scores_t) - target_t


def build_tiles(index_rows, signed_rows, slab_width):
    slabs, slot_count, user_count = index_rows.shape
    columns = jnp.arange(slab_width, dtype=jnp.float32)[None, None, :, None]
    matches = index_rows[:, :, None, :] == columns
    weight = jnp.sum(jnp.where(matches, jnp.abs(signed_rows)[:, :, None, :], 0.0), axis=1)
    target = jnp.sum(jnp.where(matches, jnp.maximum(signed_rows, 0.0)[:, :, None, :], 0.0), axis=1)
    return weight.reshape(slabs * slab_width, user_count), target.reshape(slabs * slab_width, user_count)


def per_device(user_factors, item_factors, item_index, labels, confidence):
    strata, user_count, slot_count = item_index.shape
    slab_rows, width = item_factors.shape
    signed = jnp.where(labels > 0, confidence, -confidence)
    slots_local = jnp.stack(
        [jnp.transpose(item_index.astype(jnp.float32), (0, 2, 1)), jnp.transpose(signed, (0, 2, 1))], 1
    )
    packed = jnp.concatenate([item_factors.reshape(-1), slots_local.reshape(-1)])
    gathered = gather_over(packed, "it")
    slabs = gathered.shape[0]
    cut = slab_rows * width
    block = gathered[:, :cut].reshape(slabs * slab_rows, width)
    slots_all = gathered[:, cut:].reshape((slabs,) + slots_local.shape)
    index_all = slots_all[:, :, 0]
    signed_all = slots_all[:, :, 1]

    slot_data = []
    for stratum in range(strata):
        here = jnp.stack([index_all[:, stratum], signed_all[:, stratum]], 0)
        if stratum > 0:
            here = shifted(here, "ub", stratum)
        slot_data.append(here)

    pieces = 2 if user_count % 256 == 0 else 1
    rows = user_count // pieces
    chunks = [user_factors[k * rows : (k + 1) * rows] for k in range(pieces)]
    for stratum in range(strata):
        if stratum > 0:
            chunks = [shifted(chunk, "ub", 1) for chunk in chunks]
        weight, target = build_tiles(slot_data[stratum][0], slot_data[stratum][1], slab_rows)
        finished = []
        residuals = []
        for k, chunk in enumerate(chunks):
            weight_k = weight[:, k * rows : (k + 1) * rows]
            target_k = target[:, k * rows : (k + 1) * rows]
            for inner_step in range(INNER):
                residual_t = residual_tile(chunk, block, weight_k, target_k)
                gradient = lax.dot_general(
                    residual_t, block, (((0,), (0,)), ((), ())), precision=MATMUL_PRECISION
                )
                chunk = chunk - LR_USER * (gradient + LAMBDA_REG * chunk)
            if k == 0 and stratum + 1 < strata:
                slot_data[stratum + 1], chunk = lax.optimization_barrier((slot_data[stratum + 1], chunk))
            finished.append(chunk)
            residuals.append(residual_tile(chunk, block, weight_k, target_k))
        chunks = finished
        residual_t = jnp.concatenate(residuals, 1)
        item_grad = jnp.dot(residual_t, jnp.concatenate(chunks, 0), precision=MATMUL_PRECISION)
        block = block - LR_ITEM * (item_grad + LAMBDA_REG * block)
    user_rows = jnp.concatenate([shifted(chunk, "ub", 1 - strata) for chunk in chunks], 0)
    me = lax.axis_index("it")
    slab = lax.dynamic_slice_in_dim(block, me * slab_rows, slab_rows, 0)
    return (user_rows, slab)


def solution(mesh):
    return jax.shard_map(
        per_device,
        mesh=mesh,
        in_specs=(
            P(("grp", "ub"), None),
            P(("grp", "ub", "it"), None),
            P(None, ("grp", "ub"), "it"),
            P(None, ("grp", "ub"), "it"),
            P(None, ("grp", "ub"), "it"),
        ),
        out_specs=(P(("grp", "ub"), None), P(("grp", "ub", "it"), None)),
        check_vma=False,
    )
```

```python
import jax
import jax.numpy as jnp
from jax import lax
from jax.sharding import PartitionSpec as P

INNER = 2
MATMUL_PRECISION = lax.Precision.HIGH


LR_USER = 0.02
LR_ITEM = 0.05
LAMBDA_REG = 1.0


def shifted(block, axis, distance):
    count = lax.axis_size(axis)
    route = [((i + distance) % count, i) for i in range(count)]
    return lax.ppermute(block, axis, route)


def gather_over(block, axis):
    count = lax.axis_size(axis)
    me = lax.axis_index(axis)
    received = [block] + [
        lax.ppermute(block, axis, [(i, i ^ k) for i in range(count)]) for k in range(1, count)
    ]
    order = jnp.arange(count, dtype=jnp.int32) ^ me
    return jnp.take(jnp.stack(received), order, axis=0)


def gather_line(block, axis):
    count = lax.axis_size(axis)
    if count != 4:
        return gather_over(block, axis)
    me = lax.axis_index(axis)
    from_left = lax.ppermute(block, axis, [(i, i + 1) for i in range(count - 1)])
    from_right = lax.ppermute(block, axis, [(i + 1, i) for i in range(count - 1)])
    two_left = lax.ppermute(from_left, axis, [(1, 2), (2, 3)])
    two_right = lax.ppermute(from_right, axis, [(2, 1), (1, 0)])
    three_left = lax.ppermute(from_left, axis, [(1, 3)])
    three_right = lax.ppermute(from_right, axis, [(2, 0)])
    stacked = jnp.stack([three_left, two_left, from_left, block, from_right, two_right, three_right])
    order = jnp.arange(count, dtype=jnp.int32) - me + (count - 1)
    return jnp.take(stacked, order, axis=0)


def residual_tile(user_rows, item_rows, weight_t, target_t):
    scores_t = jnp.dot(item_rows, user_rows.T, precision=MATMUL_PRECISION)
    return weight_t * jax.nn.sigmoid(scores_t) - target_t


def build_tiles(index_rows, signed_rows, slab_width):
    slabs, slot_count, user_count = index_rows.shape
    columns = jnp.arange(slab_width, dtype=jnp.float32)[None, None, :, None]
    matches = index_rows[:, :, None, :] == columns
    weight = jnp.sum(jnp.where(matches, jnp.abs(signed_rows)[:, :, None, :], 0.0), axis=1)
    target = jnp.sum(jnp.where(matches, jnp.maximum(signed_rows, 0.0)[:, :, None, :], 0.0), axis=1)
    return weight.reshape(slabs * slab_width, user_count), target.reshape(slabs * slab_width, user_count)


def per_device(user_factors, item_factors, item_index, labels, confidence):
    strata, user_count, slot_count = item_index.shape
    slab_rows, width = item_factors.shape
    signed = jnp.where(labels > 0, confidence, -confidence)
    slots_local = jnp.stack(
        [jnp.transpose(item_index.astype(jnp.float32), (0, 2, 1)), jnp.transpose(signed, (0, 2, 1))], 1
    )
    slots_all = gather_line(slots_local, "it")
    slabs = slots_all.shape[0]
    block = gather_line(item_factors, "it").reshape(slabs * slab_rows, width)
    index_all = slots_all[:, :, 0]
    signed_all = slots_all[:, :, 1]

    slot_data = []
    for stratum in range(strata):
        here = jnp.stack([index_all[:, stratum], signed_all[:, stratum]], 0)
        if stratum > 0:
            here = shifted(here, "ub", stratum)
        slot_data.append(here)

    pieces = 2 if user_count % 256 == 0 else 1
    rows = user_count // pieces
    chunks = [user_factors[k * rows : (k + 1) * rows] for k in range(pieces)]
    for stratum in range(strata):
        if stratum > 0:
            chunks = [shifted(chunk, "ub", 1) for chunk in chunks]
        weight, target = build_tiles(slot_data[stratum][0], slot_data[stratum][1], slab_rows)
        finished = []
        residuals = []
        for k, chunk in enumerate(chunks):
            weight_k = weight[:, k * rows : (k + 1) * rows]
            target_k = target[:, k * rows : (k + 1) * rows]
            for inner_step in range(INNER):
                residual_t = residual_tile(chunk, block, weight_k, target_k)
                gradient = lax.dot_general(
                    residual_t, block, (((0,), (0,)), ((), ())), precision=MATMUL_PRECISION
                )
                chunk = chunk - LR_USER * (gradient + LAMBDA_REG * chunk)
            finished.append(chunk)
            residuals.append(residual_tile(chunk, block, weight_k, target_k))
        chunks = finished
        residual_t = jnp.concatenate(residuals, 1)
        item_grad = jnp.dot(residual_t, jnp.concatenate(chunks, 0), precision=MATMUL_PRECISION)
        block = block - LR_ITEM * (item_grad + LAMBDA_REG * block)
    user_rows = jnp.concatenate([shifted(chunk, "ub", 1 - strata) for chunk in chunks], 0)
    me = lax.axis_index("it")
    slab = lax.dynamic_slice_in_dim(block, me * slab_rows, slab_rows, 0)
    return (user_rows, slab)


def solution(mesh):
    return jax.shard_map(
        per_device,
        mesh=mesh,
        in_specs=(
            P(("grp", "ub"), None),
            P(("grp", "ub", "it"), None),
            P(None, ("grp", "ub"), "it"),
            P(None, ("grp", "ub"), "it"),
            P(None, ("grp", "ub"), "it"),
        ),
        out_specs=(P(("grp", "ub"), None), P(("grp", "ub", "it"), None)),
        check_vma=False,
    )
```

```python
import jax
import jax.numpy as jnp
from jax import lax
from jax.sharding import PartitionSpec as P

INNER = 2
MATMUL_PRECISION = lax.Precision.HIGH


LR_USER = 0.02
LR_ITEM = 0.05
LAMBDA_REG = 1.0


def shifted(block, axis, distance):
    count = lax.axis_size(axis)
    route = [((i + distance) % count, i) for i in range(count)]
    return lax.ppermute(block, axis, route)


def gather_over(block, axis):
    count = lax.axis_size(axis)
    me = lax.axis_index(axis)
    received = [block] + [
        lax.ppermute(block, axis, [(i, i ^ k) for i in range(count)]) for k in range(1, count)
    ]
    order = jnp.arange(count, dtype=jnp.int32) ^ me
    return jnp.take(jnp.stack(received), order, axis=0)


def residual_tile(user_rows, item_rows, weight_t, target_t):
    scores_t = jnp.dot(item_rows, user_rows.T, precision=MATMUL_PRECISION)
    return weight_t * jax.nn.sigmoid(scores_t) - target_t


def build_tiles(index_rows, signed_rows, slab_width):
    slabs, slot_count, user_count = index_rows.shape
    columns = jnp.arange(slab_width, dtype=jnp.float32)[None, None, :, None]
    matches = index_rows[:, :, None, :] == columns
    weight = jnp.sum(jnp.where(matches, jnp.abs(signed_rows)[:, :, None, :], 0.0), axis=1)
    target = jnp.sum(jnp.where(matches, jnp.maximum(signed_rows, 0.0)[:, :, None, :], 0.0), axis=1)
    return weight.reshape(slabs * slab_width, user_count), target.reshape(slabs * slab_width, user_count)


def per_device(user_factors, item_factors, item_index, labels, confidence):
    strata, user_count, slot_count = item_index.shape
    slab_rows, width = item_factors.shape
    signed = jnp.where(labels > 0, confidence, -confidence)
    slots_local = jnp.stack(
        [jnp.transpose(item_index.astype(jnp.float32), (0, 2, 1)), jnp.transpose(signed, (0, 2, 1))], 1
    )
    slots_all = gather_over(slots_local, "it")
    slabs = slots_all.shape[0]
    block = gather_over(item_factors, "it").reshape(slabs * slab_rows, width)
    index_all = slots_all[:, :, 0]
    signed_all = slots_all[:, :, 1]

    slot_data = []
    for stratum in range(strata):
        here = jnp.stack([index_all[:, stratum], signed_all[:, stratum]], 0)
        if stratum > 0:
            here = shifted(here, "ub", stratum)
        slot_data.append(here)

    pieces = 2 if user_count % 256 == 0 else 1
    rows = user_count // pieces
    chunks = [user_factors[k * rows : (k + 1) * rows] for k in range(pieces)]
    for stratum in range(strata):
        if stratum > 0:
            chunks = [shifted(chunk, "ub", 1) for chunk in chunks]
        if stratum == strata - 1 and len(chunks) > 1:
            chunks = [jnp.concatenate(chunks, 0)]
        rows = chunks[0].shape[0]
        weight, target = build_tiles(slot_data[stratum][0], slot_data[stratum][1], slab_rows)
        finished = []
        residuals = []
        for k, chunk in enumerate(chunks):
            weight_k = weight[:, k * rows : (k + 1) * rows]
            target_k = target[:, k * rows : (k + 1) * rows]
            for inner_step in range(INNER):
                residual_t = residual_tile(chunk, block, weight_k, target_k)
                gradient = lax.dot_general(
                    residual_t, block, (((0,), (0,)), ((), ())), precision=MATMUL_PRECISION
                )
                chunk = chunk - LR_USER * (gradient + LAMBDA_REG * chunk)
            finished.append(chunk)
            residuals.append(residual_tile(chunk, block, weight_k, target_k))
        chunks = finished
        residual_t = jnp.concatenate(residuals, 1)
        item_grad = jnp.dot(residual_t, jnp.concatenate(chunks, 0), precision=MATMUL_PRECISION)
        block = block - LR_ITEM * (item_grad + LAMBDA_REG * block)
    user_rows = jnp.concatenate([shifted(chunk, "ub", 1 - strata) for chunk in chunks], 0)
    me = lax.axis_index("it")
    slab = lax.dynamic_slice_in_dim(block, me * slab_rows, slab_rows, 0)
    return (user_rows, slab)


def solution(mesh):
    return jax.shard_map(
        per_device,
        mesh=mesh,
        in_specs=(
            P(("grp", "ub"), None),
            P(("grp", "ub", "it"), None),
            P(None, ("grp", "ub"), "it"),
            P(None, ("grp", "ub"), "it"),
            P(None, ("grp", "ub"), "it"),
        ),
        out_specs=(P(("grp", "ub"), None), P(("grp", "ub", "it"), None)),
        check_vma=False,
    )
```

```python
import jax
import jax.numpy as jnp
from jax import lax
from jax.sharding import PartitionSpec as P

INNER = 2
MATMUL_PRECISION = lax.Precision.HIGH


LR_USER = 0.02
LR_ITEM = 0.05
LAMBDA_REG = 1.0


def shifted(block, axis, distance):
    count = lax.axis_size(axis)
    route = [((i + distance) % count, i) for i in range(count)]
    return lax.ppermute(block, axis, route)


def gather_over(block, axis):
    count = lax.axis_size(axis)
    me = lax.axis_index(axis)
    received = [block] + [
        lax.ppermute(block, axis, [(i, i ^ k) for i in range(count)]) for k in range(1, count)
    ]
    order = jnp.arange(count, dtype=jnp.int32) ^ me
    return jnp.take(jnp.stack(received), order, axis=0)


def residual_tile(user_rows, item_rows, weight_t, target_t):
    scores_t = jnp.dot(item_rows, user_rows.T, precision=MATMUL_PRECISION)
    return weight_t * jax.nn.sigmoid(scores_t) - target_t


def build_tiles(index_rows, signed_rows, slab_width):
    slabs, slot_count, user_count = index_rows.shape
    columns = jnp.arange(slab_width, dtype=jnp.float32)[None, None, :, None]
    matches = index_rows[:, :, None, :] == columns
    weight = jnp.sum(jnp.where(matches, jnp.abs(signed_rows)[:, :, None, :], 0.0), axis=1)
    target = jnp.sum(jnp.where(matches, jnp.maximum(signed_rows, 0.0)[:, :, None, :], 0.0), axis=1)
    return weight.reshape(slabs * slab_width, user_count), target.reshape(slabs * slab_width, user_count)


def per_device(user_factors, item_factors, item_index, labels, confidence):
    strata, user_count, slot_count = item_index.shape
    slab_rows, width = item_factors.shape
    signed = jnp.where(labels > 0, confidence, -confidence)
    index_t = jnp.transpose(item_index.astype(jnp.float32), (0, 2, 1))
    half = slot_count // 2
    index_pairs = index_t[:, :half] + 256.0 * index_t[:, half:]
    slots_local = jnp.concatenate([jnp.transpose(signed, (0, 2, 1)), index_pairs], 1)
    slots_all = gather_over(slots_local, "it")
    slabs = slots_all.shape[0]
    block = gather_over(item_factors, "it").reshape(slabs * slab_rows, width)
    high = jnp.floor(slots_all[:, :, slot_count:] * (1.0 / 256.0))
    low = slots_all[:, :, slot_count:] - 256.0 * high
    index_all = jnp.concatenate([low, high], 2)
    signed_all = slots_all[:, :, :slot_count]

    slot_data = []
    for stratum in range(strata):
        here = jnp.stack([index_all[:, stratum], signed_all[:, stratum]], 0)
        if stratum > 0:
            here = shifted(here, "ub", stratum)
        slot_data.append(here)

    pieces = 2 if user_count % 256 == 0 else 1
    rows = user_count // pieces
    chunks = [user_factors[k * rows : (k + 1) * rows] for k in range(pieces)]
    for stratum in range(strata):
        if stratum > 0:
            chunks = [shifted(chunk, "ub", 1) for chunk in chunks]
        weight, target = build_tiles(slot_data[stratum][0], slot_data[stratum][1], slab_rows)
        finished = []
        residuals = []
        for k, chunk in enumerate(chunks):
            weight_k = weight[:, k * rows : (k + 1) * rows]
            target_k = target[:, k * rows : (k + 1) * rows]
            for inner_step in range(INNER):
                residual_t = residual_tile(chunk, block, weight_k, target_k)
                gradient = lax.dot_general(
                    residual_t, block, (((0,), (0,)), ((), ())), precision=MATMUL_PRECISION
                )
                chunk = chunk - LR_USER * (gradient + LAMBDA_REG * chunk)
            finished.append(chunk)
            residuals.append(residual_tile(chunk, block, weight_k, target_k))
        chunks = finished
        residual_t = jnp.concatenate(residuals, 1)
        item_grad = jnp.dot(residual_t, jnp.concatenate(chunks, 0), precision=MATMUL_PRECISION)
        block = block - LR_ITEM * (item_grad + LAMBDA_REG * block)
    user_rows = jnp.concatenate([shifted(chunk, "ub", 1 - strata) for chunk in chunks], 0)
    me = lax.axis_index("it")
    slab = lax.dynamic_slice_in_dim(block, me * slab_rows, slab_rows, 0)
    return (user_rows, slab)


def solution(mesh):
    return jax.shard_map(
        per_device,
        mesh=mesh,
        in_specs=(
            P(("grp", "ub"), None),
            P(("grp", "ub", "it"), None),
            P(None, ("grp", "ub"), "it"),
            P(None, ("grp", "ub"), "it"),
            P(None, ("grp", "ub"), "it"),
        ),
        out_specs=(P(("grp", "ub"), None), P(("grp", "ub", "it"), None)),
        check_vma=False,
    )
```

```python
import jax
import jax.numpy as jnp
from jax import lax
from jax.sharding import PartitionSpec as P

INNER = 2
MATMUL_PRECISION = lax.Precision.HIGH


LR_USER = 0.02
LR_ITEM = 0.05
LAMBDA_REG = 1.0


def shifted(block, axis, distance):
    count = lax.axis_size(axis)
    route = [((i + distance) % count, i) for i in range(count)]
    return lax.ppermute(block, axis, route)


def gather_over(block, axis):
    count = lax.axis_size(axis)
    me = lax.axis_index(axis)
    received = [block] + [
        lax.ppermute(block, axis, [(i, i ^ k) for i in range(count)]) for k in range(1, count)
    ]
    order = jnp.arange(count, dtype=jnp.int32) ^ me
    return jnp.take(jnp.stack(received), order, axis=0)


def residual_tile(user_rows, item_rows, weight_t, target_t):
    scores_t = jnp.dot(item_rows, user_rows.T, precision=MATMUL_PRECISION)
    return weight_t * jax.nn.sigmoid(scores_t) - target_t


def build_tiles(index_rows, signed_rows, slab_width):
    slabs, slot_count, user_count = index_rows.shape
    columns = jnp.arange(slab_width, dtype=jnp.float32)[None, None, :, None]
    matches = index_rows[:, :, None, :] == columns
    weight = jnp.sum(jnp.where(matches, jnp.abs(signed_rows)[:, :, None, :], 0.0), axis=1)
    target = jnp.sum(jnp.where(matches, jnp.maximum(signed_rows, 0.0)[:, :, None, :], 0.0), axis=1)
    return weight.reshape(slabs * slab_width, user_count), target.reshape(slabs * slab_width, user_count)


def per_device(user_factors, item_factors, item_index, labels, confidence):
    strata, user_count, slot_count = item_index.shape
    slab_rows, width = item_factors.shape
    signed = jnp.where(labels > 0, confidence, -confidence)
    index_t = jnp.transpose(item_index.astype(jnp.float32), (0, 2, 1))
    half = slot_count // 2
    index_pairs = index_t[:, :half] + 256.0 * index_t[:, half:]
    slots_local = jnp.concatenate([jnp.transpose(signed, (0, 2, 1)), index_pairs], 1)
    slots_all = gather_over(slots_local, "it")
    slabs = slots_all.shape[0]
    slots_all, item_factors = lax.optimization_barrier((slots_all, item_factors))
    block = gather_over(item_factors, "it").reshape(slabs * slab_rows, width)
    high = jnp.floor(slots_all[:, :, slot_count:] * (1.0 / 256.0))
    low = slots_all[:, :, slot_count:] - 256.0 * high
    index_all = jnp.concatenate([low, high], 2)
    signed_all = slots_all[:, :, :slot_count]

    slot_data = []
    for stratum in range(strata):
        here = jnp.stack([index_all[:, stratum], signed_all[:, stratum]], 0)
        if stratum > 0:
            here = shifted(here, "ub", stratum)
        slot_data.append(here)

    pieces = 2 if user_count % 256 == 0 else 1
    rows = user_count // pieces
    chunks = [user_factors[k * rows : (k + 1) * rows] for k in range(pieces)]
    for stratum in range(strata):
        if stratum > 0:
            chunks = [shifted(chunk, "ub", 1) for chunk in chunks]
        weight, target = build_tiles(slot_data[stratum][0], slot_data[stratum][1], slab_rows)
        finished = []
        residuals = []
        for k, chunk in enumerate(chunks):
            weight_k = weight[:, k * rows : (k + 1) * rows]
            target_k = target[:, k * rows : (k + 1) * rows]
            for inner_step in range(INNER):
                residual_t = residual_tile(chunk, block, weight_k, target_k)
                gradient = lax.dot_general(
                    residual_t, block, (((0,), (0,)), ((), ())), precision=MATMUL_PRECISION
                )
                chunk = chunk - LR_USER * (gradient + LAMBDA_REG * chunk)
            finished.append(chunk)
            residuals.append(residual_tile(chunk, block, weight_k, target_k))
        chunks = finished
        residual_t = jnp.concatenate(residuals, 1)
        item_grad = jnp.dot(residual_t, jnp.concatenate(chunks, 0), precision=MATMUL_PRECISION)
        block = block - LR_ITEM * (item_grad + LAMBDA_REG * block)
    user_rows = jnp.concatenate([shifted(chunk, "ub", 1 - strata) for chunk in chunks], 0)
    me = lax.axis_index("it")
    slab = lax.dynamic_slice_in_dim(block, me * slab_rows, slab_rows, 0)
    return (user_rows, slab)


def solution(mesh):
    return jax.shard_map(
        per_device,
        mesh=mesh,
        in_specs=(
            P(("grp", "ub"), None),
            P(("grp", "ub", "it"), None),
            P(None, ("grp", "ub"), "it"),
            P(None, ("grp", "ub"), "it"),
            P(None, ("grp", "ub"), "it"),
        ),
        out_specs=(P(("grp", "ub"), None), P(("grp", "ub", "it"), None)),
        check_vma=False,
    )
```

```python
import jax
import jax.numpy as jnp
from jax import lax
from jax.sharding import PartitionSpec as P

INNER = 2
MATMUL_PRECISION = lax.Precision.HIGH


LR_USER = 0.02
LR_ITEM = 0.05
LAMBDA_REG = 1.0


def shifted(block, axis, distance):
    count = lax.axis_size(axis)
    route = [((i + distance) % count, i) for i in range(count)]
    return lax.ppermute(block, axis, route)


def gather_over(block, axis):
    count = lax.axis_size(axis)
    me = lax.axis_index(axis)
    received = [block] + [
        lax.ppermute(block, axis, [(i, i ^ k) for i in range(count)]) for k in range(1, count)
    ]
    order = jnp.arange(count, dtype=jnp.int32) ^ me
    return jnp.take(jnp.stack(received), order, axis=0)


def residual_tile(user_rows, item_rows, weight_t, target_t):
    scores_t = jnp.dot(item_rows, user_rows.T, precision=MATMUL_PRECISION)
    return weight_t * (0.5 * jnp.tanh(0.5 * scores_t) + 0.5) - target_t


def build_tiles(index_rows, signed_rows, slab_width):
    slabs, slot_count, user_count = index_rows.shape
    columns = jnp.arange(slab_width, dtype=jnp.float32)[None, None, :, None]
    matches = index_rows[:, :, None, :] == columns
    weight = jnp.sum(jnp.where(matches, jnp.abs(signed_rows)[:, :, None, :], 0.0), axis=1)
    target = jnp.sum(jnp.where(matches, jnp.maximum(signed_rows, 0.0)[:, :, None, :], 0.0), axis=1)
    return weight.reshape(slabs * slab_width, user_count), target.reshape(slabs * slab_width, user_count)


def per_device(user_factors, item_factors, item_index, labels, confidence):
    strata, user_count, slot_count = item_index.shape
    slab_rows, width = item_factors.shape
    signed = jnp.where(labels > 0, confidence, -confidence)
    slots_local = jnp.stack(
        [jnp.transpose(item_index.astype(jnp.float32), (0, 2, 1)), jnp.transpose(signed, (0, 2, 1))], 1
    )
    slots_all = gather_over(slots_local, "it")
    slabs = slots_all.shape[0]
    block = gather_over(item_factors, "it").reshape(slabs * slab_rows, width)
    index_all = slots_all[:, :, 0]
    signed_all = slots_all[:, :, 1]

    slot_data = []
    for stratum in range(strata):
        here = jnp.stack([index_all[:, stratum], signed_all[:, stratum]], 0)
        if stratum > 0:
            here = shifted(here, "ub", stratum)
        slot_data.append(here)

    pieces = 2 if user_count % 256 == 0 else 1
    rows = user_count // pieces
    chunks = [user_factors[k * rows : (k + 1) * rows] for k in range(pieces)]
    for stratum in range(strata):
        if stratum > 0:
            chunks = [shifted(chunk, "ub", 1) for chunk in chunks]
        weight, target = build_tiles(slot_data[stratum][0], slot_data[stratum][1], slab_rows)
        finished = []
        residuals = []
        for k, chunk in enumerate(chunks):
            weight_k = weight[:, k * rows : (k + 1) * rows]
            target_k = target[:, k * rows : (k + 1) * rows]
            for inner_step in range(INNER):
                residual_t = residual_tile(chunk, block, weight_k, target_k)
                gradient = lax.dot_general(
                    residual_t, block, (((0,), (0,)), ((), ())), precision=MATMUL_PRECISION
                )
                chunk = chunk - LR_USER * (gradient + LAMBDA_REG * chunk)
            finished.append(chunk)
            residuals.append(residual_tile(chunk, block, weight_k, target_k))
        chunks = finished
        residual_t = jnp.concatenate(residuals, 1)
        item_grad = jnp.dot(residual_t, jnp.concatenate(chunks, 0), precision=MATMUL_PRECISION)
        block = block - LR_ITEM * (item_grad + LAMBDA_REG * block)
    user_rows = jnp.concatenate([shifted(chunk, "ub", 1 - strata) for chunk in chunks], 0)
    me = lax.axis_index("it")
    slab = lax.dynamic_slice_in_dim(block, me * slab_rows, slab_rows, 0)
    return (user_rows, slab)


def solution(mesh):
    return jax.shard_map(
        per_device,
        mesh=mesh,
        in_specs=(
            P(("grp", "ub"), None),
            P(("grp", "ub", "it"), None),
            P(None, ("grp", "ub"), "it"),
            P(None, ("grp", "ub"), "it"),
            P(None, ("grp", "ub"), "it"),
        ),
        out_specs=(P(("grp", "ub"), None), P(("grp", "ub", "it"), None)),
        check_vma=False,
    )
```

```python
import jax
import jax.numpy as jnp
from jax import lax
from jax.sharding import PartitionSpec as P

INNER = 2
MATMUL_PRECISION = lax.Precision.HIGH


LR_USER = 0.02
LR_ITEM = 0.05
LAMBDA_REG = 1.0


def shifted(block, axis, distance):
    count = lax.axis_size(axis)
    route = [((i + distance) % count, i) for i in range(count)]
    return lax.ppermute(block, axis, route)


def gather_over(block, axis):
    count = lax.axis_size(axis)
    me = lax.axis_index(axis)
    received = [block] + [
        lax.ppermute(block, axis, [(i, i ^ k) for i in range(count)]) for k in range(1, count)
    ]
    order = jnp.arange(count, dtype=jnp.int32) ^ me
    return jnp.take(jnp.stack(received), order, axis=0)


def residual_tile(user_rows, item_rows, weight_t, target_t):
    scores_t = jnp.dot(item_rows, user_rows.T, precision=MATMUL_PRECISION)
    return weight_t * jax.nn.sigmoid(scores_t) - target_t


def build_tiles(index_rows, signed_rows, slab_width):
    slabs, slot_count, user_count = index_rows.shape
    columns = jnp.arange(slab_width, dtype=jnp.float32)[None, None, :, None]
    matches = index_rows[:, :, None, :] == columns
    weight = jnp.sum(jnp.where(matches, jnp.abs(signed_rows)[:, :, None, :], 0.0), axis=1)
    target = jnp.sum(jnp.where(matches, jnp.maximum(signed_rows, 0.0)[:, :, None, :], 0.0), axis=1)
    return weight.reshape(slabs * slab_width, user_count), target.reshape(slabs * slab_width, user_count)


def per_device(user_factors, item_factors, item_index, labels, confidence):
    strata, user_count, slot_count = item_index.shape
    slab_rows, width = item_factors.shape
    signed = jnp.where(labels > 0, confidence, -confidence)
    slots_local = jnp.stack(
        [jnp.transpose(item_index.astype(jnp.float32), (0, 2, 1)), jnp.transpose(signed, (0, 2, 1))], 1
    )
    slots_all = lax.all_gather(slots_local, "it")
    slabs = slots_all.shape[0]
    block = gather_over(item_factors, "it").reshape(slabs * slab_rows, width)
    index_all = slots_all[:, :, 0]
    signed_all = slots_all[:, :, 1]

    slot_data = []
    for stratum in range(strata):
        here = jnp.stack([index_all[:, stratum], signed_all[:, stratum]], 0)
        if stratum > 0:
            here = shifted(here, "ub", stratum)
        slot_data.append(here)

    pieces = 2 if user_count % 256 == 0 else 1
    rows = user_count // pieces
    chunks = [user_factors[k * rows : (k + 1) * rows] for k in range(pieces)]
    for stratum in range(strata):
        if stratum > 0:
            chunks = [shifted(chunk, "ub", 1) for chunk in chunks]
        weight, target = build_tiles(slot_data[stratum][0], slot_data[stratum][1], slab_rows)
        finished = []
        residuals = []
        for k, chunk in enumerate(chunks):
            weight_k = weight[:, k * rows : (k + 1) * rows]
            target_k = target[:, k * rows : (k + 1) * rows]
            for inner_step in range(INNER):
                residual_t = residual_tile(chunk, block, weight_k, target_k)
                gradient = lax.dot_general(
                    residual_t, block, (((0,), (0,)), ((), ())), precision=MATMUL_PRECISION
                )
                chunk = chunk - LR_USER * (gradient + LAMBDA_REG * chunk)
            finished.append(chunk)
            residuals.append(residual_tile(chunk, block, weight_k, target_k))
        chunks = finished
        residual_t = jnp.concatenate(residuals, 1)
        item_grad = jnp.dot(residual_t, jnp.concatenate(chunks, 0), precision=MATMUL_PRECISION)
        block = block - LR_ITEM * (item_grad + LAMBDA_REG * block)
    user_rows = jnp.concatenate([shifted(chunk, "ub", 1 - strata) for chunk in chunks], 0)
    me = lax.axis_index("it")
    slab = lax.dynamic_slice_in_dim(block, me * slab_rows, slab_rows, 0)
    return (user_rows, slab)


def solution(mesh):
    return jax.shard_map(
        per_device,
        mesh=mesh,
        in_specs=(
            P(("grp", "ub"), None),
            P(("grp", "ub", "it"), None),
            P(None, ("grp", "ub"), "it"),
            P(None, ("grp", "ub"), "it"),
            P(None, ("grp", "ub"), "it"),
        ),
        out_specs=(P(("grp", "ub"), None), P(("grp", "ub", "it"), None)),
        check_vma=False,
    )
```

```python
import jax
import jax.numpy as jnp
from jax import lax
from jax.sharding import PartitionSpec as P

INNER = 2
MATMUL_PRECISION = lax.Precision.HIGH


LR_USER = 0.02
LR_ITEM = 0.05
LAMBDA_REG = 1.0


def shifted(block, axis, distance):
    count = lax.axis_size(axis)
    route = [((i + distance) % count, i) for i in range(count)]
    return lax.ppermute(block, axis, route)


def gather_over(block, axis):
    count = lax.axis_size(axis)
    me = lax.axis_index(axis)
    received = [block] + [
        lax.ppermute(block, axis, [(i, i ^ k) for i in range(count)]) for k in range(1, count)
    ]
    order = jnp.arange(count, dtype=jnp.int32) ^ me
    return jnp.take(jnp.stack(received), order, axis=0)


def gather_both(slab, slots, axis):
    count = lax.axis_size(axis)
    me = lax.axis_index(axis)
    flat_slab, flat_slots = slab.reshape(-1), slots.reshape(-1)
    slab_from, slots_from = [flat_slab], [flat_slots]
    for k in range(1, count):
        pairs = [(i, i ^ k) for i in range(count)]
        if k == 1:
            both = lax.ppermute(jnp.concatenate([flat_slots, flat_slab]), axis, pairs)
            slots_from.append(both[: flat_slots.size])
            slab_from.append(both[flat_slots.size :])
        else:
            slots_from.append(lax.ppermute(flat_slots, axis, pairs))
            slab_from.append(lax.ppermute(flat_slab, axis, pairs))
    order = jnp.arange(count, dtype=jnp.int32) ^ me
    slots_all = jnp.take(jnp.stack(slots_from), order, axis=0)
    return jnp.stack(slab_from), order, slots_all.reshape((count,) + slots.shape)


def residual_tile(user_rows, item_rows, weight_t, target_t):
    scores_t = jnp.dot(item_rows, user_rows.T, precision=MATMUL_PRECISION)
    return weight_t * jax.nn.sigmoid(scores_t) - target_t


def build_tiles(index_rows, signed_rows, slab_width):
    slabs, slot_count, user_count = index_rows.shape
    columns = jnp.arange(slab_width, dtype=jnp.float32)[None, None, :, None]
    matches = index_rows[:, :, None, :] == columns
    weight = jnp.sum(jnp.where(matches, jnp.abs(signed_rows)[:, :, None, :], 0.0), axis=1)
    target = jnp.sum(jnp.where(matches, jnp.maximum(signed_rows, 0.0)[:, :, None, :], 0.0), axis=1)
    return weight.reshape(slabs * slab_width, user_count), target.reshape(slabs * slab_width, user_count)


def per_device(user_factors, item_factors, item_index, labels, confidence):
    strata, user_count, slot_count = item_index.shape
    slab_rows, width = item_factors.shape
    signed = jnp.where(labels > 0, confidence, -confidence)
    slots_local = jnp.stack(
        [jnp.transpose(item_index.astype(jnp.float32), (0, 2, 1)), jnp.transpose(signed, (0, 2, 1))], 1
    )
    slab_stack, order, slots_all = gather_both(item_factors, slots_local, "it")
    slabs = slots_all.shape[0]
    index_all = slots_all[:, :, 0]
    signed_all = slots_all[:, :, 1]

    slot_data = []
    for stratum in range(strata):
        here = jnp.stack([index_all[:, stratum], signed_all[:, stratum]], 0)
        if stratum > 0:
            here = shifted(here, "ub", stratum)
        slot_data.append(here)

    pieces = 2 if user_count % 256 == 0 else 1
    rows = user_count // pieces
    chunks = [user_factors[k * rows : (k + 1) * rows] for k in range(pieces)]
    for stratum in range(strata):
        if stratum > 0:
            chunks = [shifted(chunk, "ub", 1) for chunk in chunks]
        weight, target = build_tiles(slot_data[stratum][0], slot_data[stratum][1], slab_rows)
        if stratum == 0:
            slab_stack, weight, target = lax.optimization_barrier((slab_stack, weight, target))
            block = jnp.take(slab_stack, order, axis=0).reshape(slabs * slab_rows, width)
        finished = []
        residuals = []
        for k, chunk in enumerate(chunks):
            weight_k = weight[:, k * rows : (k + 1) * rows]
            target_k = target[:, k * rows : (k + 1) * rows]
            for inner_step in range(INNER):
                residual_t = residual_tile(chunk, block, weight_k, target_k)
                gradient = lax.dot_general(
                    residual_t, block, (((0,), (0,)), ((), ())), precision=MATMUL_PRECISION
                )
                chunk = chunk - LR_USER * (gradient + LAMBDA_REG * chunk)
            finished.append(chunk)
            residuals.append(residual_tile(chunk, block, weight_k, target_k))
        chunks = finished
        residual_t = jnp.concatenate(residuals, 1)
        item_grad = jnp.dot(residual_t, jnp.concatenate(chunks, 0), precision=MATMUL_PRECISION)
        block = block - LR_ITEM * (item_grad + LAMBDA_REG * block)
    user_rows = jnp.concatenate([shifted(chunk, "ub", 1 - strata) for chunk in chunks], 0)
    me = lax.axis_index("it")
    slab = lax.dynamic_slice_in_dim(block, me * slab_rows, slab_rows, 0)
    return (user_rows, slab)


def solution(mesh):
    return jax.shard_map(
        per_device,
        mesh=mesh,
        in_specs=(
            P(("grp", "ub"), None),
            P(("grp", "ub", "it"), None),
            P(None, ("grp", "ub"), "it"),
            P(None, ("grp", "ub"), "it"),
            P(None, ("grp", "ub"), "it"),
        ),
        out_specs=(P(("grp", "ub"), None), P(("grp", "ub", "it"), None)),
        check_vma=False,
    )
```

```python
import jax
import jax.numpy as jnp
from jax import lax
from jax.sharding import PartitionSpec as P

INNER = 2
MATMUL_PRECISION = lax.Precision.HIGH


LR_USER = 0.02
LR_ITEM = 0.05
LAMBDA_REG = 1.0


def shifted(block, axis, distance):
    count = lax.axis_size(axis)
    route = [((i + distance) % count, i) for i in range(count)]
    return lax.ppermute(block, axis, route)


def gather_over(block, axis):
    count = lax.axis_size(axis)
    me = lax.axis_index(axis)
    received = [block] + [
        lax.ppermute(block, axis, [(i, i ^ k) for i in range(count)]) for k in range(1, count)
    ]
    order = jnp.arange(count, dtype=jnp.int32) ^ me
    return jnp.take(jnp.stack(received), order, axis=0)


def residual_tile(user_rows, item_rows, weight_t, target_t):
    scores_t = jnp.dot(item_rows, user_rows.T, precision=MATMUL_PRECISION)
    return weight_t * jax.nn.sigmoid(scores_t) - target_t


def residual_tile_t(user_cols, item_rows, weight_t, target_t):
    scores_t = jnp.dot(item_rows, user_cols, precision=MATMUL_PRECISION)
    return weight_t * jax.nn.sigmoid(scores_t) - target_t


def build_tiles(index_rows, signed_rows, slab_width):
    slabs, slot_count, user_count = index_rows.shape
    columns = jnp.arange(slab_width, dtype=jnp.float32)[None, None, :, None]
    matches = index_rows[:, :, None, :] == columns
    weight = jnp.sum(jnp.where(matches, jnp.abs(signed_rows)[:, :, None, :], 0.0), axis=1)
    target = jnp.sum(jnp.where(matches, jnp.maximum(signed_rows, 0.0)[:, :, None, :], 0.0), axis=1)
    return weight.reshape(slabs * slab_width, user_count), target.reshape(slabs * slab_width, user_count)


def per_device(user_factors, item_factors, item_index, labels, confidence):
    strata, user_count, slot_count = item_index.shape
    slab_rows, width = item_factors.shape
    signed = jnp.where(labels > 0, confidence, -confidence)
    slots_local = jnp.stack(
        [jnp.transpose(item_index.astype(jnp.float32), (0, 2, 1)), jnp.transpose(signed, (0, 2, 1))], 1
    )
    slots_all = gather_over(slots_local, "it")
    slabs = slots_all.shape[0]
    block = gather_over(item_factors, "it").reshape(slabs * slab_rows, width)
    index_all = slots_all[:, :, 0]
    signed_all = slots_all[:, :, 1]

    slot_data = []
    for stratum in range(strata):
        here = jnp.stack([index_all[:, stratum], signed_all[:, stratum]], 0)
        if stratum > 0:
            here = shifted(here, "ub", stratum)
        slot_data.append(here)

    pieces = 2 if user_count % 256 == 0 else 1
    rows = user_count // pieces
    chunks = [user_factors[k * rows : (k + 1) * rows].T for k in range(pieces)]
    for stratum in range(strata):
        if stratum > 0:
            chunks = [shifted(chunk, "ub", 1) for chunk in chunks]
        weight, target = build_tiles(slot_data[stratum][0], slot_data[stratum][1], slab_rows)
        block_t = block.T
        finished = []
        residuals = []
        for k, chunk in enumerate(chunks):
            weight_k = weight[:, k * rows : (k + 1) * rows]
            target_k = target[:, k * rows : (k + 1) * rows]
            for inner_step in range(INNER):
                residual_t = residual_tile_t(chunk, block, weight_k, target_k)
                gradient_t = jnp.dot(block_t, residual_t, precision=MATMUL_PRECISION)
                chunk = chunk - LR_USER * (gradient_t + LAMBDA_REG * chunk)
            finished.append(chunk)
            residuals.append(residual_tile_t(chunk, block, weight_k, target_k))
        chunks = finished
        residual_t = jnp.concatenate(residuals, 1)
        item_grad = lax.dot_general(
            residual_t, jnp.concatenate(chunks, 1), (((1,), (1,)), ((), ())), precision=MATMUL_PRECISION
        )
        block = block - LR_ITEM * (item_grad + LAMBDA_REG * block)
    user_rows = jnp.concatenate([shifted(chunk, "ub", 1 - strata) for chunk in chunks], 1).T
    me = lax.axis_index("it")
    slab = lax.dynamic_slice_in_dim(block, me * slab_rows, slab_rows, 0)
    return (user_rows, slab)


def solution(mesh):
    return jax.shard_map(
        per_device,
        mesh=mesh,
        in_specs=(
            P(("grp", "ub"), None),
            P(("grp", "ub", "it"), None),
            P(None, ("grp", "ub"), "it"),
            P(None, ("grp", "ub"), "it"),
            P(None, ("grp", "ub"), "it"),
        ),
        out_specs=(P(("grp", "ub"), None), P(("grp", "ub", "it"), None)),
        check_vma=False,
    )
```

```python
import jax
import jax.numpy as jnp
from jax import lax
from jax.sharding import PartitionSpec as P

INNER = 2
MATMUL_PRECISION = lax.Precision.HIGH


LR_USER = 0.02
LR_ITEM = 0.05
LAMBDA_REG = 1.0


def shifted(block, axis, distance):
    count = lax.axis_size(axis)
    route = [((i + distance) % count, i) for i in range(count)]
    return lax.ppermute(block, axis, route)


def gather_over(block, axis):
    count = lax.axis_size(axis)
    me = lax.axis_index(axis)
    received = [block] + [
        lax.ppermute(block, axis, [(i, i ^ k) for i in range(count)]) for k in range(1, count)
    ]
    order = jnp.arange(count, dtype=jnp.int32) ^ me
    return jnp.take(jnp.stack(received), order, axis=0)


def residual_tile(user_rows, item_rows, weight_t, target_t):
    scores_t = jnp.dot(item_rows, user_rows.T, precision=MATMUL_PRECISION)
    return weight_t * jax.nn.sigmoid(scores_t) - target_t


def build_tiles(index_rows, signed_rows, slab_width):
    slabs, slot_count, user_count = index_rows.shape
    columns = jnp.arange(slab_width, dtype=jnp.float32)[None, None, :, None]
    matches = index_rows[:, :, None, :] == columns
    weight = jnp.sum(jnp.where(matches, jnp.abs(signed_rows)[:, :, None, :], 0.0), axis=1)
    target = jnp.sum(jnp.where(matches, jnp.maximum(signed_rows, 0.0)[:, :, None, :], 0.0), axis=1)
    return weight.reshape(slabs * slab_width, user_count), target.reshape(slabs * slab_width, user_count)


def per_device(user_factors, item_factors, item_index, labels, confidence):
    strata, user_count, slot_count = item_index.shape
    slab_rows, width = item_factors.shape
    signed = jnp.where(labels > 0, confidence, -confidence)
    slots_local = jnp.stack(
        [jnp.transpose(item_index.astype(jnp.float32), (0, 2, 1)), jnp.transpose(signed, (0, 2, 1))], 1
    )
    slots_all = gather_over(slots_local, "it")
    slabs = slots_all.shape[0]
    block = gather_over(item_factors, "it").reshape(slabs * slab_rows, width)
    index_all = slots_all[:, :, 0]
    signed_all = slots_all[:, :, 1]

    slot_data = []
    for stratum in range(strata):
        here = jnp.stack([index_all[:, stratum], signed_all[:, stratum]], 0)
        if stratum > 0:
            here = shifted(here, "ub", stratum)
        slot_data.append(here)

    pieces = 2 if user_count % 256 == 0 else 1
    rows = user_count // pieces
    chunks = [user_factors[k * rows : (k + 1) * rows] for k in range(pieces)]
    for stratum in range(strata):
        if stratum > 0:
            chunks = [shifted(chunk, "ub", 1) for chunk in chunks]
        weight, target = build_tiles(slot_data[stratum][0], slot_data[stratum][1], slab_rows)
        finished = []
        residuals = []
        for k, chunk in enumerate(chunks):
            weight_k = weight[:, k * rows : (k + 1) * rows]
            target_k = target[:, k * rows : (k + 1) * rows]
            for inner_step in range(INNER):
                residual_t = residual_tile(chunk, block, weight_k, target_k)
                gradient = lax.dot_general(
                    residual_t, block, (((0,), (0,)), ((), ())), precision=MATMUL_PRECISION
                )
                chunk = chunk - LR_USER * (gradient + LAMBDA_REG * chunk)
            if k == 0 and stratum + 2 == strata:
                slot_data[stratum + 1], chunk = lax.optimization_barrier((slot_data[stratum + 1], chunk))
            finished.append(chunk)
            residuals.append(residual_tile(chunk, block, weight_k, target_k))
        chunks = finished
        residual_t = jnp.concatenate(residuals, 1)
        item_grad = jnp.dot(residual_t, jnp.concatenate(chunks, 0), precision=MATMUL_PRECISION)
        block = block - LR_ITEM * (item_grad + LAMBDA_REG * block)
    user_rows = jnp.concatenate([shifted(chunk, "ub", 1 - strata) for chunk in chunks], 0)
    me = lax.axis_index("it")
    slab = lax.dynamic_slice_in_dim(block, me * slab_rows, slab_rows, 0)
    return (user_rows, slab)


def solution(mesh):
    return jax.shard_map(
        per_device,
        mesh=mesh,
        in_specs=(
            P(("grp", "ub"), None),
            P(("grp", "ub", "it"), None),
            P(None, ("grp", "ub"), "it"),
            P(None, ("grp", "ub"), "it"),
            P(None, ("grp", "ub"), "it"),
        ),
        out_specs=(P(("grp", "ub"), None), P(("grp", "ub", "it"), None)),
        check_vma=False,
    )
```

```python
import jax
import jax.numpy as jnp
from jax import lax
from jax.sharding import PartitionSpec as P

INNER = 2
MATMUL_PRECISION = lax.Precision.HIGH


LR_USER = 0.02
LR_ITEM = 0.05
LAMBDA_REG = 1.0


def shifted(block, axis, distance):
    count = lax.axis_size(axis)
    route = [((i + distance) % count, i) for i in range(count)]
    return lax.ppermute(block, axis, route)


def gather_over(block, axis):
    count = lax.axis_size(axis)
    me = lax.axis_index(axis)
    received = [block] + [
        lax.ppermute(block, axis, [(i, i ^ k) for i in range(count)]) for k in range(1, count)
    ]
    order = jnp.arange(count, dtype=jnp.int32) ^ me
    return jnp.take(jnp.stack(received), order, axis=0)


def residual_tile(user_rows, item_rows, weight_t, target_t):
    scores_t = jnp.dot(item_rows, user_rows.T, precision=MATMUL_PRECISION)
    return weight_t * jax.nn.sigmoid(scores_t) - target_t


def build_tiles(index_rows, signed_rows, slab_width):
    slabs, slot_count, user_count = index_rows.shape
    columns = jnp.arange(slab_width, dtype=jnp.float32)[None, None, :, None]
    matches = index_rows[:, :, None, :] == columns
    weight = jnp.sum(jnp.where(matches, jnp.abs(signed_rows)[:, :, None, :], 0.0), axis=1)
    target = jnp.sum(jnp.where(matches, jnp.maximum(signed_rows, 0.0)[:, :, None, :], 0.0), axis=1)
    return weight.reshape(slabs * slab_width, user_count), target.reshape(slabs * slab_width, user_count)


def per_device(user_factors, item_factors, item_index, labels, confidence):
    strata, user_count, slot_count = item_index.shape
    slab_rows, width = item_factors.shape
    signed = jnp.where(labels > 0, confidence, -confidence)
    slots_local = jnp.stack(
        [jnp.transpose(item_index.astype(jnp.float32), (0, 2, 1)), jnp.transpose(signed, (0, 2, 1))], 1
    )
    slots_all = gather_over(slots_local, "it")
    slabs = slots_all.shape[0]
    block = gather_over(item_factors, "it").reshape(slabs * slab_rows, width)
    index_all = slots_all[:, :, 0]
    signed_all = slots_all[:, :, 1]

    slot_data = []
    for stratum in range(strata):
        here = jnp.stack([index_all[:, stratum], signed_all[:, stratum]], 0)
        if stratum > 0:
            here = shifted(here, "ub", stratum)
        slot_data.append(here)

    pieces = 2 if user_count % 256 == 0 else 1
    rows = user_count // pieces
    chunks = [user_factors[k * rows : (k + 1) * rows] for k in range(pieces)]
    for stratum in range(strata):
        if stratum > 0:
            chunks = [shifted(chunk, "ub", 1) for chunk in chunks]
        weight, target = build_tiles(slot_data[stratum][0], slot_data[stratum][1], slab_rows)
        finished = []
        residuals = []
        for k, chunk in enumerate(chunks):
            weight_k = weight[:, k * rows : (k + 1) * rows]
            target_k = target[:, k * rows : (k + 1) * rows]
            for inner_step in range(INNER):
                residual_t = residual_tile(chunk, block, weight_k, target_k)
                gradient = lax.dot_general(
                    residual_t, block, (((0,), (0,)), ((), ())), precision=MATMUL_PRECISION
                )
                chunk = chunk - LR_USER * (gradient + LAMBDA_REG * chunk)
            finished.append(chunk)
            residuals.append(residual_tile(chunk, block, weight_k, target_k))
        chunks = finished
        residual_t = jnp.concatenate(residuals, 1)
        item_grad = jnp.dot(residual_t, jnp.concatenate(chunks, 0), precision=MATMUL_PRECISION)
        block = block - LR_ITEM * (item_grad + LAMBDA_REG * block)
    user_rows = shifted(jnp.concatenate(chunks, 0), "ub", 1 - strata)
    me = lax.axis_index("it")
    slab = lax.dynamic_slice_in_dim(block, me * slab_rows, slab_rows, 0)
    return (user_rows, slab)


def solution(mesh):
    return jax.shard_map(
        per_device,
        mesh=mesh,
        in_specs=(
            P(("grp", "ub"), None),
            P(("grp", "ub", "it"), None),
            P(None, ("grp", "ub"), "it"),
            P(None, ("grp", "ub"), "it"),
            P(None, ("grp", "ub"), "it"),
        ),
        out_specs=(P(("grp", "ub"), None), P(("grp", "ub", "it"), None)),
        check_vma=False,
    )
```
